256 devices in a mesh: seq: 32 (over z, y), head: 8 (over x, core).
Axes of the slice: x: 4, y: 4, z: 8, core: 2. Of those that a mesh axis runs over, the one named last changes fastest.
Arguments:
- x_in: bfloat16 [16384, 5120], P('seq', 'head'), may hold values from -6 to 6
- z_gate: bfloat16 [16384, 5120], P('seq', 'head'), may hold values from -6 to 6
- step_size: float32 [80, 16384], P('head', 'seq'), may hold values from 0.005 to 0.05
- log_decay: float32 [80, 16384], P('head', 'seq'), may hold values from -1 to 0
- b_proj: bfloat16 [16384, 128], P('seq'), may hold values from -6 to 6
- c_proj: bfloat16 [16384, 128], P('seq'), may hold values from -0.5 to 0.5
- d_skip: float32 [80], P('head'), may hold values from 0.5 to 1.5
- norm_weight: float32 [5120], P('head'), may hold values from 0.5 to 1.5
- w_out: bfloat16 [5120, 2560], P('head'), may hold values from -0.125 to 0.125
- resid: bfloat16 [2560, 16384], P('head', 'seq'), may hold values from -6 to 6
- masked_pos: int32 [8192], P('seq'), may hold values from 0 to 16383, as said below
- owner: int32 [8192], P('seq'), may hold values from 0 to 31, as said below
Outputs:
- block_out: bfloat16 [2560, 16384], P('head', 'seq')
- targets: bfloat16 [2560, 16384], P('head', 'seq')
The draws below stay inside these ranges and needn't reach their ends.
Inputs may be any that keep to these rules, and one draw needn't show every extreme that they name: `masked_pos`: the 256 entries listed by device i of seq are distinct positions from i * 512 to (i + 1) * 512 - 1. Among the 256 entries of each device of seq, no owner is named more than 16 times; one owner, the same for all devices, is named exactly 16 times by each device.
All inputs are finite; a program needn't handle non-finite values.
Results may differ from the reference program's by a relative error of at most 0.025.
Values may be sent and summed in bfloat16 or wider, within the bound.
No kernel may reach another device: no remote copies, remote signals or barrier semaphores. Data moves between devices by JAX's collectives and lax.ppermute only.
A program may use at most 64 MiB of HBM per device.

```python
import math
import jax
import jax.numpy as jnp
from jax import lax

D = 2560
HEAD_DIM = 64
STATE = 128
BLOCK = 256
HEADS_DEV = 10
TOK_DEV = 512
SCAN_HEADS = 80
SEQUENCE_TOKENS = 16384
MASK_DEV = 256
CAP = 16
MASKED = 8192
SLOTS = 16384
N_SEQ = 32
N_HEAD = 8


def draw_log_decay(key, part):
    random_keys = jax.random.split(key, 7)
    share = 0.5
    fast = jax.random.uniform(random_keys[0], (SCAN_HEADS,)) < share
    fast_rate = jnp.exp(jax.random.uniform(random_keys[1], (SCAN_HEADS,), jnp.float32, math.log(1.0 / 50.0), math.log(1.0 / 30.0)))
    slow_rate = 0.4 / SEQUENCE_TOKENS * jnp.exp(jax.random.uniform(random_keys[2], (SCAN_HEADS,), jnp.float32, math.log(0.5), math.log(1.5)))
    base = jnp.where(fast, fast_rate, slow_rate)
    devices = SEQUENCE_TOKENS // TOK_DEV
    factor = jnp.exp(jax.random.uniform(random_keys[3], (SCAN_HEADS, devices), jnp.float32, math.log(0.7), math.log(1.4)))
    factor = jnp.repeat(factor, TOK_DEV, axis=1)
    rough = jax.random.uniform(random_keys[4], (SCAN_HEADS, SEQUENCE_TOKENS), jnp.float32, 0.5, 1.5)
    span_begin = jax.random.randint(random_keys[5], (SCAN_HEADS, 2), 0, SEQUENCE_TOKENS)
    span_length = jax.random.uniform(random_keys[6], (SCAN_HEADS, 2), jnp.float32, 0.22, 0.69)
    target_positions = jnp.arange(SEQUENCE_TOKENS, dtype=jnp.int32)
    matched_count = (target_positions[None, None, :] == span_begin[:, :, None]).astype(jnp.float32)
    additional = jnp.sum(matched_count * span_length[:, :, None], axis=1)
    return (-(base[:, None] * factor * rough + additional)).astype(jnp.float32)


def draw_masked_pos(key, part):
    devices = MASKED // MASK_DEV

    def one_device(number):
        picked = jax.random.permutation(jax.random.fold_in(key, number), TOK_DEV)[:MASK_DEV]
        return picked + number * TOK_DEV
    listed = jax.vmap(one_device)(jnp.arange(devices, dtype=jnp.int32))
    return listed.reshape(MASKED).astype(jnp.int32)


def draw_owner(key, part):
    devices = MASKED // MASK_DEV
    hot = jax.random.randint(jax.random.fold_in(key, 7), (), 0, devices)

    def one_device(number):
        device_key = jax.random.fold_in(key, number + 100)
        first_key, second_key = jax.random.split(device_key)
        slot_ids = jax.random.permutation(first_key, (devices - 1) * CAP)[:MASK_DEV - CAP]
        others = slot_ids // CAP
        others = others + (others >= hot).astype(jnp.int32)
        owners = jnp.concatenate([jnp.full((CAP,), hot, jnp.int32), others.astype(jnp.int32)])
        return jax.random.permutation(second_key, owners)
    listed = jax.vmap(one_device)(jnp.arange(devices, dtype=jnp.int32))
    return listed.reshape(MASKED).astype(jnp.int32)


def with_spikes(values, key, source, target, blocks, factor):
    owner, partner = [(jnp.arange(values.shape[axis_at]) // (values.shape[axis_at] // blocks)).reshape([-1 if axis == axis_at else 1 for axis in range(values.ndim)]) for axis_at in (source, target)]
    chosen = jax.random.permutation(key, blocks)[partner]
    strong = (owner == chosen) | (owner == (partner + blocks // 2) % blocks)
    return jnp.where(strong, factor * values, values)


def levels(rng, extent, shards, low, largest):
    gain, own = 1.0, jax.random.fold_in(rng, 6)
    for position, blocks in shards:
        draws = jnp.exp(jax.random.uniform(jax.random.fold_in(own, position), (blocks,), jnp.float32, low / len(shards), largest / len(shards)))
        gain = gain * jnp.repeat(draws, extent[position] // blocks).reshape([-1 if axis == position else 1 for axis in range(len(extent))])
    return gain


def scatter_about(own_key, dims, deviation, most, cuts=(), kind=jnp.bfloat16):
    gain = levels(own_key, dims, cuts, -0.22, 0.18) if cuts else 1.0
    values = jax.random.normal(own_key, dims, jnp.float32) * deviation * gain
    return jnp.minimum(jnp.maximum(values, -most), most).astype(kind)


def noise_with(rng, extent, deviation, reach, pieces, heavy, kind=jnp.bfloat16):
    values = deviation * jax.random.normal(rng, extent, jnp.float32)
    if pieces:
        values = values * levels(rng, extent, pieces, -0.22, 0.18)
    return jnp.clip(with_spikes(values, jax.random.fold_in(rng, 3), *heavy), -reach, reach).astype(kind)


def setup_inputs(seed: int = 0) -> dict:
    key_list = jax.random.split(jax.random.key(seed), 13)
    x_in = scatter_about(key_list[0], (SEQUENCE_TOKENS, SCAN_HEADS * HEAD_DIM), 1.0, 6.0, ((0, 32), (1, 8)))
    z_gate = scatter_about(key_list[1], (SEQUENCE_TOKENS, SCAN_HEADS * HEAD_DIM), 1.0, 6.0, ((0, 32), (1, 8)))
    step_size = jnp.clip(jnp.exp(math.log(0.05) - 2.3025851 * jax.random.uniform(key_list[2], (SCAN_HEADS, SEQUENCE_TOKENS), jnp.float32) ** levels(key_list[2], (SCAN_HEADS, SEQUENCE_TOKENS), ((0, 8), (1, 32)), -0.2, 0.2)), 0.005, 0.05)
    log_decay = draw_log_decay(jax.random.fold_in(key_list[12], 71), 0)
    b_proj = scatter_about(key_list[4], (SEQUENCE_TOKENS, STATE), 1.0, 6.0, ((0, 32),))
    c_proj = scatter_about(key_list[5], (SEQUENCE_TOKENS, STATE), STATE ** -0.5, 0.5, ((0, 32),))
    d_skip = jnp.clip(0.5 + 1.0 * jax.random.uniform(key_list[6], (SCAN_HEADS,), jnp.float32) ** levels(key_list[6], (SCAN_HEADS,), ((0, 8),), -0.2, 0.2), 0.5, 1.5)
    norm_weight = jnp.clip(1.0 + 0.1 * jax.random.normal(key_list[7], (SCAN_HEADS * HEAD_DIM,), jnp.float32), 0.5, 1.5)
    w_out = noise_with(key_list[8], (SCAN_HEADS * HEAD_DIM, D), (SCAN_HEADS * HEAD_DIM) ** -0.5, 0.125, ((0, 8),), (0, 1, 8, 2.0))
    resid = scatter_about(key_list[9], (D, SEQUENCE_TOKENS), 1.0, 6.0, ((0, 8), (1, 32)))
    masked_pos = draw_masked_pos(jax.random.fold_in(key_list[12], 71), 0)
    owner = draw_owner(jax.random.fold_in(key_list[12], 71), 0)
    return dict(x_in=x_in, z_gate=z_gate, step_size=step_size, log_decay=log_decay, b_proj=b_proj, c_proj=c_proj, d_skip=d_skip, norm_weight=norm_weight, w_out=w_out, resid=resid, masked_pos=masked_pos, owner=owner)


EPS = 1e-05

def reference(x_in, z_gate, step_size, log_decay, b_proj, c_proj, d_skip, norm_weight, w_out, resid, masked_pos, owner):
    blocks = SEQUENCE_TOKENS // BLOCK
    x_all = x_in.reshape(blocks, BLOCK, SCAN_HEADS, HEAD_DIM)
    b_all = b_proj.reshape(blocks, BLOCK, STATE)
    c_all = c_proj.reshape(blocks, BLOCK, STATE)
    dt_all = jnp.transpose(step_size.reshape(SCAN_HEADS, blocks, BLOCK), (1, 0, 2))
    cum_all = jnp.cumsum(jnp.transpose(log_decay.reshape(SCAN_HEADS, blocks, BLOCK), (1, 0, 2)), axis=-1)
    lower = jnp.arange(BLOCK)[:, None] >= jnp.arange(BLOCK)[None, :]

    def advance(state, inputs):
        x_blk, b_blk, c_blk, dt_blk, cum_blk = inputs
        gram = jnp.dot(c_blk, b_blk.T, preferred_element_type=jnp.float32)
        spread = cum_blk[:, :, None] - cum_blk[:, None, :]
        decay = jnp.where(lower[None], jnp.exp(jnp.where(lower[None], spread, 0.0)), 0.0)
        weights = (gram[None] * decay * dt_blk[:, None, :]).astype(jnp.bfloat16)
        x_wide = x_blk.astype(jnp.float32)
        inner = jnp.einsum('hts,shp->thp', weights.astype(jnp.float32), x_wide)
        end_weight = jnp.exp(cum_blk[:, -1:] - cum_blk) * dt_blk
        keyed = (end_weight[:, :, None] * b_blk.astype(jnp.float32)[None]).astype(jnp.bfloat16)
        block_state = jnp.einsum('hsn,shp->hpn', keyed.astype(jnp.float32), x_wide)
        carried = jnp.einsum('tn,hpn->thp', c_blk.astype(jnp.float32), state, precision=lax.Precision.HIGHEST)
        carried = carried * jnp.exp(cum_blk).T[:, :, None]
        result = inner + carried + d_skip[None, :, None] * x_wide
        new_state = jnp.exp(cum_blk[:, -1])[:, None, None] * state + block_state
        return (new_state, result)
    start_state = jnp.zeros((SCAN_HEADS, HEAD_DIM, STATE), jnp.float32)
    _, results = lax.scan(advance, start_state, (x_all, b_all, c_all, dt_all, cum_all))
    mixed = results.reshape(SEQUENCE_TOKENS, SCAN_HEADS * HEAD_DIM)
    gated = mixed * jax.nn.silu(z_gate.astype(jnp.float32))
    mean_sq = lax.optimization_barrier(jnp.mean(gated * gated, axis=-1, keepdims=True))
    hidden = (gated * lax.rsqrt(mean_sq + EPS) * norm_weight[None, :]).astype(jnp.bfloat16)
    group = HEADS_DEV * HEAD_DIM
    proj = jnp.zeros((D, SEQUENCE_TOKENS), jnp.float32)
    for member in range(N_HEAD):
        part = jnp.dot(w_out[member * group:(member + 1) * group].T, hidden[:, member * group:(member + 1) * group].T, preferred_element_type=jnp.float32)
        rounded = lax.optimization_barrier(part.astype(jnp.bfloat16))
        proj = proj + rounded.astype(jnp.float32)
    block_out = (resid.astype(jnp.float32) + proj).astype(jnp.bfloat16)
    column = block_out.astype(jnp.float32)
    mean_col = lax.optimization_barrier(jnp.mean(column, axis=0))
    variance = lax.optimization_barrier(jnp.mean(column * column, axis=0)) - mean_col * mean_col
    normed = ((column - mean_col[None, :]) * lax.rsqrt(variance + EPS)[None, :]).astype(jnp.bfloat16)
    owner_hot = (owner[:, None] == jnp.arange(N_SEQ, dtype=jnp.int32)[None, :]).astype(jnp.int32)
    owner_hot = owner_hot.reshape(N_SEQ, MASK_DEV, N_SEQ)
    earlier = jnp.cumsum(owner_hot, axis=1) - owner_hot
    ranks = lax.optimization_barrier(jnp.sum(earlier * owner_hot, axis=-1)).reshape(MASKED).astype(jnp.int32)
    source = (jnp.arange(MASKED, dtype=jnp.int32) // MASK_DEV).astype(jnp.int32)
    placed = (owner * (N_SEQ * CAP) + source * CAP + ranks).astype(jnp.int32)
    targets = jnp.zeros((D, SLOTS), jnp.bfloat16).at[:, placed].set(normed[:, masked_pos])
    return (block_out, targets)
```

```python
import jax
import jax.numpy as jnp
from jax import lax
from jax.sharding import PartitionSpec as P

BLOCK = 256


EPS = 1e-05


def from_behind(value, axis, steps):
    count = lax.axis_size(axis)
    leading, last = (max(0, -steps), min(count, count - steps))
    return lax.ppermute(value, axis, [(source, source + steps) for source in range(leading, last)])


def body(
    x_in,
    z_gate,
    step_size,
    log_decay,
    b_proj,
    c_proj,
    d_skip,
    norm_weight,
    w_out,
    resid,
    masked_pos,
    owner,
):
    rows_here = x_in.shape[0]
    heads_here = step_size.shape[0]
    channels = x_in.shape[1]
    head_size = channels // heads_here
    state_size = b_proj.shape[1]
    blocks = rows_here // BLOCK
    x_all = x_in.reshape(blocks, BLOCK, heads_here, head_size)
    b_all = b_proj.reshape(blocks, BLOCK, state_size)
    c_all = c_proj.reshape(blocks, BLOCK, state_size)
    dt_all = step_size.reshape(heads_here, blocks, BLOCK)
    cum_all = jnp.cumsum(log_decay.reshape(heads_here, blocks, BLOCK), axis=-1)
    lower = jnp.arange(BLOCK)[:, None] >= jnp.arange(BLOCK)[None, :]
    gram = jnp.einsum("ctn,csn->cts", c_all, b_all, preferred_element_type=jnp.float32)
    spread = cum_all[:, :, :, None] - cum_all[:, :, None, :]
    decay = jnp.where(lower[None, None], jnp.exp(jnp.where(lower[None, None], spread, 0.0)), 0.0)
    weights = (gram[None] * decay * dt_all[:, :, None, :]).astype(jnp.bfloat16)
    inner = jnp.einsum("hcts,cshp->cthp", weights, x_all, preferred_element_type=jnp.float32)
    end_weight = jnp.exp(cum_all[:, :, -1:] - cum_all) * dt_all
    keyed = (end_weight[..., None] * b_all.astype(jnp.float32)[None]).astype(jnp.bfloat16)
    block_states = jnp.einsum("hcsn,cshp->chpn", keyed, x_all, preferred_element_type=jnp.float32)
    block_decay = jnp.exp(cum_all[:, :, -1])
    running = jnp.zeros((heads_here, head_size, state_size), jnp.float32)
    reach = jnp.ones((heads_here,), jnp.float32)
    starts = []
    reaches = []
    for number in range(blocks):
        starts.append(running)
        reaches.append(reach)
        running = block_decay[:, number][:, None, None] * running + block_states[number]
        reach = reach * block_decay[:, number]
    seq_count = lax.axis_size("seq")
    me = lax.axis_index("seq")
    log_total = jnp.sum(cum_all[:, :, -1], axis=1)
    all_states = lax.all_gather(running.astype(jnp.bfloat16), "seq", tiled=False)
    all_logs = lax.all_gather(log_total, "seq", tiled=False)
    index = jnp.arange(seq_count)
    between = (index[:, None] < index[None, :]) & (index[None, :] < me)
    spans = jnp.sum(jnp.where(between[:, :, None], all_logs[None, :, :], 0.0), axis=1)
    gains = jnp.where((index < me)[:, None], jnp.exp(spans), 0.0)
    incoming = jnp.einsum(
        "jh,jhpn->hpn",
        gains,
        all_states.astype(jnp.float32),
        precision=lax.Precision.HIGHEST,
        preferred_element_type=jnp.float32,
    )
    start_states = jnp.stack(starts) + jnp.stack(reaches)[:, :, None, None] * incoming[None]
    carried = jnp.einsum(
        "ctn,chpn->cthp",
        c_all.astype(jnp.float32),
        start_states,
        precision=lax.Precision.HIGHEST,
        preferred_element_type=jnp.float32,
    )
    carried = carried * jnp.transpose(jnp.exp(cum_all), (1, 2, 0))[:, :, :, None]
    mixed = inner + carried + d_skip[None, None, :, None] * x_all.astype(jnp.float32)
    mixed = mixed.reshape(rows_here, channels)
    gated = mixed * jax.nn.silu(z_gate.astype(jnp.float32))
    squares = lax.psum(jnp.sum(gated * gated, axis=-1), "head")
    mean_sq = squares / (channels * lax.axis_size("head"))
    hidden = (gated * lax.rsqrt(mean_sq + EPS)[:, None] * norm_weight[None, :]).astype(jnp.bfloat16)
    proj = lax.psum_scatter(
        jnp.einsum("kd,tk->dt", w_out, hidden, preferred_element_type=jnp.float32).astype(
            jnp.bfloat16
        ),
        "head",
        scatter_dimension=0,
        tiled=True,
    ).astype(jnp.float32)
    block_out = (resid.astype(jnp.float32) + proj).astype(jnp.bfloat16)
    features = resid.shape[0] * lax.axis_size("head")
    masked_here = masked_pos.shape[0]
    slot_cap = 2 * masked_here // seq_count
    local_pos = masked_pos % rows_here
    owner_hot = (owner[:, None] == jnp.arange(seq_count, dtype=jnp.int32)[None, :]).astype(
        jnp.bfloat16
    )
    strictly = (jnp.arange(masked_here)[:, None] > jnp.arange(masked_here)[None, :]).astype(
        jnp.bfloat16
    )
    earlier = jnp.dot(strictly, owner_hot, preferred_element_type=jnp.float32)
    ranks = jnp.sum(earlier * owner_hot.astype(jnp.float32), axis=-1).astype(jnp.int32)
    placed = owner * slot_cap + ranks
    local_feat = resid.shape[0]
    out_wide = block_out.astype(jnp.float32)
    totals = lax.psum((jnp.sum(out_wide, axis=0), jnp.sum(out_wide * out_wide, axis=0)), "head")
    mean_col = totals[0] / features
    variance = totals[1] / features - mean_col * mean_col
    normed = ((out_wide - mean_col[None, :]) * lax.rsqrt(variance + EPS)[None, :]).astype(
        jnp.bfloat16
    )
    buffer = (
        jnp.zeros((local_feat, seq_count * slot_cap), jnp.bfloat16)
        .at[:, placed]
        .set(normed[:, local_pos])
    )
    received = lax.all_to_all(
        buffer.reshape(local_feat, seq_count, slot_cap),
        "seq",
        split_axis=1,
        concat_axis=1,
        tiled=True,
    )
    targets = received.reshape(local_feat, seq_count * slot_cap)
    return (block_out, targets)


def solution(mesh):
    placed = (
        P("seq", "head"),
        P("seq", "head"),
        P("head", "seq"),
        P("head", "seq"),
        P("seq", None),
        P("seq", None),
        P("head"),
        P("head"),
        P("head", None),
        P("head", "seq"),
        P("seq"),
        P("seq"),
    )
    return jax.shard_map(
        body,
        mesh=mesh,
        in_specs=placed,
        out_specs=(P("head", "seq"), P("head", "seq")),
        check_vma=False,
    )
```

```python
import jax
import jax.numpy as jnp
from jax import lax
from jax.sharding import PartitionSpec as P

BLOCK = 256


EPS = 1e-05


def from_behind(value, axis, steps):
    count = lax.axis_size(axis)
    leading, last = (max(0, -steps), min(count, count - steps))
    return lax.ppermute(value, axis, [(source, source + steps) for source in range(leading, last)])


def body(
    x_in,
    z_gate,
    step_size,
    log_decay,
    b_proj,
    c_proj,
    d_skip,
    norm_weight,
    w_out,
    resid,
    masked_pos,
    owner,
):
    rows_here = x_in.shape[0]
    heads_here = step_size.shape[0]
    channels = x_in.shape[1]
    head_size = channels // heads_here
    state_size = b_proj.shape[1]
    blocks = rows_here // BLOCK
    x_all = x_in.reshape(blocks, BLOCK, heads_here, head_size)
    b_all = b_proj.reshape(blocks, BLOCK, state_size)
    c_all = c_proj.reshape(blocks, BLOCK, state_size)
    dt_all = step_size.reshape(heads_here, blocks, BLOCK)
    cum_all = jnp.cumsum(log_decay.reshape(heads_here, blocks, BLOCK), axis=-1)
    lower = jnp.arange(BLOCK)[:, None] >= jnp.arange(BLOCK)[None, :]
    gram = jnp.einsum("ctn,csn->cts", c_all, b_all, preferred_element_type=jnp.float32)
    spread = cum_all[:, :, :, None] - cum_all[:, :, None, :]
    decay = jnp.where(lower[None, None], jnp.exp(jnp.where(lower[None, None], spread, 0.0)), 0.0)
    weights = (gram[None] * decay * dt_all[:, :, None, :]).astype(jnp.bfloat16)
    inner = jnp.einsum("hcts,cshp->cthp", weights, x_all, preferred_element_type=jnp.float32)
    end_weight = jnp.exp(cum_all[:, :, -1:] - cum_all) * dt_all
    keyed = (end_weight[..., None] * b_all.astype(jnp.float32)[None]).astype(jnp.bfloat16)
    block_states = jnp.einsum("hcsn,cshp->chpn", keyed, x_all, preferred_element_type=jnp.float32)
    block_decay = jnp.exp(cum_all[:, :, -1])
    running = jnp.zeros((heads_here, head_size, state_size), jnp.float32)
    reach = jnp.ones((heads_here,), jnp.float32)
    starts = []
    reaches = []
    for number in range(blocks):
        starts.append(running)
        reaches.append(reach)
        running = block_decay[:, number][:, None, None] * running + block_states[number]
        reach = reach * block_decay[:, number]
    seq_count = lax.axis_size("seq")
    me = lax.axis_index("seq")
    log_total = jnp.sum(cum_all[:, :, -1], axis=1)
    high = lax.reduce_precision(log_total, exponent_bits=8, mantissa_bits=7)
    rest = log_total - high
    middle = lax.reduce_precision(rest, exponent_bits=8, mantissa_bits=7)
    low = rest - middle
    spare = jnp.zeros((16, state_size), jnp.float32)
    spare = spare.at[0:3, 0:heads_here].set(jnp.stack([high, middle, low]))
    slab = jnp.concatenate(
        [running.reshape(heads_here * head_size, state_size), spare], axis=0
    ).astype(jnp.bfloat16)
    gathered = lax.all_gather(slab, "seq", tiled=False)
    all_states = gathered[:, : heads_here * head_size].reshape(
        seq_count, heads_here, head_size, state_size
    )
    all_logs = jnp.sum(
        gathered[:, heads_here * head_size : heads_here * head_size + 3, :heads_here].astype(
            jnp.float32
        ),
        axis=1,
    )
    index = jnp.arange(seq_count)
    between = (index[:, None] < index[None, :]) & (index[None, :] < me)
    spans = jnp.sum(jnp.where(between[:, :, None], all_logs[None, :, :], 0.0), axis=1)
    gains = jnp.where((index < me)[:, None], jnp.exp(spans), 0.0)
    incoming = jnp.einsum(
        "jh,jhpn->hpn",
        gains,
        all_states.astype(jnp.float32),
        precision=lax.Precision.HIGHEST,
        preferred_element_type=jnp.float32,
    )
    start_states = jnp.stack(starts) + jnp.stack(reaches)[:, :, None, None] * incoming[None]
    carried = jnp.einsum(
        "ctn,chpn->cthp",
        c_all.astype(jnp.float32),
        start_states,
        precision=lax.Precision.HIGHEST,
        preferred_element_type=jnp.float32,
    )
    carried = carried * jnp.transpose(jnp.exp(cum_all), (1, 2, 0))[:, :, :, None]
    mixed = inner + carried + d_skip[None, None, :, None] * x_all.astype(jnp.float32)
    mixed = mixed.reshape(rows_here, channels)
    gated = mixed * jax.nn.silu(z_gate.astype(jnp.float32))
    squares = lax.psum(jnp.sum(gated * gated, axis=-1), "head")
    mean_sq = squares / (channels * lax.axis_size("head"))
    hidden = (gated * lax.rsqrt(mean_sq + EPS)[:, None] * norm_weight[None, :]).astype(jnp.bfloat16)
    proj = lax.psum_scatter(
        jnp.einsum("kd,tk->dt", w_out, hidden, preferred_element_type=jnp.float32).astype(
            jnp.bfloat16
        ),
        "head",
        scatter_dimension=0,
        tiled=True,
    ).astype(jnp.float32)
    block_out = (resid.astype(jnp.float32) + proj).astype(jnp.bfloat16)
    features = resid.shape[0] * lax.axis_size("head")
    masked_here = masked_pos.shape[0]
    slot_cap = 2 * masked_here // seq_count
    local_pos = masked_pos % rows_here
    owner_hot = (owner[:, None] == jnp.arange(seq_count, dtype=jnp.int32)[None, :]).astype(
        jnp.bfloat16
    )
    strictly = (jnp.arange(masked_here)[:, None] > jnp.arange(masked_here)[None, :]).astype(
        jnp.bfloat16
    )
    earlier = jnp.dot(strictly, owner_hot, preferred_element_type=jnp.float32)
    ranks = jnp.sum(earlier * owner_hot.astype(jnp.float32), axis=-1).astype(jnp.int32)
    placed = owner * slot_cap + ranks
    local_feat = resid.shape[0]
    out_wide = block_out.astype(jnp.float32)
    totals = lax.psum((jnp.sum(out_wide, axis=0), jnp.sum(out_wide * out_wide, axis=0)), "head")
    mean_col = totals[0] / features
    variance = totals[1] / features - mean_col * mean_col
    normed = ((out_wide - mean_col[None, :]) * lax.rsqrt(variance + EPS)[None, :]).astype(
        jnp.bfloat16
    )
    buffer = (
        jnp.zeros((local_feat, seq_count * slot_cap), jnp.bfloat16)
        .at[:, placed]
        .set(normed[:, local_pos])
    )
    received = lax.all_to_all(
        buffer.reshape(local_feat, seq_count, slot_cap),
        "seq",
        split_axis=1,
        concat_axis=1,
        tiled=True,
    )
    targets = received.reshape(local_feat, seq_count * slot_cap)
    return (block_out, targets)


def solution(mesh):
    placed = (
        P("seq", "head"),
        P("seq", "head"),
        P("head", "seq"),
        P("head", "seq"),
        P("seq", None),
        P("seq", None),
        P("head"),
        P("head"),
        P("head", None),
        P("head", "seq"),
        P("seq"),
        P("seq"),
    )
    return jax.shard_map(
        body,
        mesh=mesh,
        in_specs=placed,
        out_specs=(P("head", "seq"), P("head", "seq")),
        check_vma=False,
    )
```

```python
import jax
import jax.numpy as jnp
from jax import lax
from jax.sharding import PartitionSpec as P

BLOCK = 256


EPS = 1e-05


def from_behind(value, axis, steps):
    count = lax.axis_size(axis)
    leading, last = (max(0, -steps), min(count, count - steps))
    return lax.ppermute(value, axis, [(source, source + steps) for source in range(leading, last)])


def body(
    x_in,
    z_gate,
    step_size,
    log_decay,
    b_proj,
    c_proj,
    d_skip,
    norm_weight,
    w_out,
    resid,
    masked_pos,
    owner,
):
    rows_here = x_in.shape[0]
    heads_here = step_size.shape[0]
    channels = x_in.shape[1]
    head_size = channels // heads_here
    state_size = b_proj.shape[1]
    blocks = rows_here // BLOCK
    x_all = x_in.reshape(blocks, BLOCK, heads_here, head_size)
    b_all = b_proj.reshape(blocks, BLOCK, state_size)
    c_all = c_proj.reshape(blocks, BLOCK, state_size)
    dt_all = step_size.reshape(heads_here, blocks, BLOCK)
    cum_all = jnp.cumsum(log_decay.reshape(heads_here, blocks, BLOCK), axis=-1)
    lower = jnp.arange(BLOCK)[:, None] >= jnp.arange(BLOCK)[None, :]
    gram = jnp.einsum("ctn,csn->cts", c_all, b_all, preferred_element_type=jnp.float32)
    spread = cum_all[:, :, :, None] - cum_all[:, :, None, :]
    decay = jnp.where(lower[None, None], jnp.exp(jnp.where(lower[None, None], spread, 0.0)), 0.0)
    weights = (gram[None] * decay * dt_all[:, :, None, :]).astype(jnp.bfloat16)
    inner = jnp.einsum("hcts,cshp->cthp", weights, x_all, preferred_element_type=jnp.float32)
    end_weight = jnp.exp(cum_all[:, :, -1:] - cum_all) * dt_all
    keyed = (end_weight[..., None] * b_all.astype(jnp.float32)[None]).astype(jnp.bfloat16)
    block_states = jnp.einsum("hcsn,cshp->chpn", keyed, x_all, preferred_element_type=jnp.float32)
    block_decay = jnp.exp(cum_all[:, :, -1])
    running = jnp.zeros((heads_here, head_size, state_size), jnp.float32)
    reach = jnp.ones((heads_here,), jnp.float32)
    starts = []
    reaches = []
    for number in range(blocks):
        starts.append(running)
        reaches.append(reach)
        running = block_decay[:, number][:, None, None] * running + block_states[number]
        reach = reach * block_decay[:, number]
    seq_count = lax.axis_size("seq")
    log_total = jnp.sum(cum_all[:, :, -1], axis=1)
    rows = heads_here * head_size

    def pack(logs, state):
        high = lax.reduce_precision(logs, exponent_bits=8, mantissa_bits=7)
        rest = logs - high
        middle = lax.reduce_precision(rest, exponent_bits=8, mantissa_bits=7)
        spare = jnp.zeros((16, state_size), jnp.float32)
        spare = spare.at[0:3, 0:heads_here].set(jnp.stack([high, middle, rest - middle]))
        return jnp.concatenate([state.reshape(rows, state_size), spare], axis=0).astype(
            jnp.bfloat16
        )

    def unpack(slab):
        wide = slab.astype(jnp.float32)
        logs = jnp.sum(wide[rows : rows + 3, :heads_here], axis=0)
        return logs, wide[:rows].reshape(heads_here, head_size, state_size)

    logs, state = unpack(from_behind(pack(log_total, running), "seq", 1))
    distance = 1
    while distance < seq_count:
        earlier_logs, earlier_state = unpack(from_behind(pack(logs, state), "seq", distance))
        state = jnp.exp(logs)[:, None, None] * earlier_state + state
        logs = logs + earlier_logs
        distance *= 2
    incoming = state
    start_states = jnp.stack(starts) + jnp.stack(reaches)[:, :, None, None] * incoming[None]
    carried = jnp.einsum(
        "ctn,chpn->cthp",
        c_all.astype(jnp.float32),
        start_states,
        precision=lax.Precision.HIGHEST,
        preferred_element_type=jnp.float32,
    )
    carried = carried * jnp.transpose(jnp.exp(cum_all), (1, 2, 0))[:, :, :, None]
    mixed = inner + carried + d_skip[None, None, :, None] * x_all.astype(jnp.float32)
    mixed = mixed.reshape(rows_here, channels)
    gated = mixed * jax.nn.silu(z_gate.astype(jnp.float32))
    squares = lax.psum(jnp.sum(gated * gated, axis=-1), "head")
    mean_sq = squares / (channels * lax.axis_size("head"))
    hidden = (gated * lax.rsqrt(mean_sq + EPS)[:, None] * norm_weight[None, :]).astype(jnp.bfloat16)
    proj = lax.psum_scatter(
        jnp.einsum("kd,tk->dt", w_out, hidden, preferred_element_type=jnp.float32).astype(
            jnp.bfloat16
        ),
        "head",
        scatter_dimension=0,
        tiled=True,
    ).astype(jnp.float32)
    block_out = (resid.astype(jnp.float32) + proj).astype(jnp.bfloat16)
    features = resid.shape[0] * lax.axis_size("head")
    masked_here = masked_pos.shape[0]
    slot_cap = 2 * masked_here // seq_count
    local_pos = masked_pos % rows_here
    owner_hot = (owner[:, None] == jnp.arange(seq_count, dtype=jnp.int32)[None, :]).astype(
        jnp.bfloat16
    )
    strictly = (jnp.arange(masked_here)[:, None] > jnp.arange(masked_here)[None, :]).astype(
        jnp.bfloat16
    )
    earlier = jnp.dot(strictly, owner_hot, preferred_element_type=jnp.float32)
    ranks = jnp.sum(earlier * owner_hot.astype(jnp.float32), axis=-1).astype(jnp.int32)
    placed = owner * slot_cap + ranks
    local_feat = resid.shape[0]
    out_wide = block_out.astype(jnp.float32)
    totals = lax.psum((jnp.sum(out_wide, axis=0), jnp.sum(out_wide * out_wide, axis=0)), "head")
    mean_col = totals[0] / features
    variance = totals[1] / features - mean_col * mean_col
    normed = ((out_wide - mean_col[None, :]) * lax.rsqrt(variance + EPS)[None, :]).astype(
        jnp.bfloat16
    )
    buffer = (
        jnp.zeros((local_feat, seq_count * slot_cap), jnp.bfloat16)
        .at[:, placed]
        .set(normed[:, local_pos])
    )
    received = lax.all_to_all(
        buffer.reshape(local_feat, seq_count, slot_cap),
        "seq",
        split_axis=1,
        concat_axis=1,
        tiled=True,
    )
    targets = received.reshape(local_feat, seq_count * slot_cap)
    return (block_out, targets)


def solution(mesh):
    placed = (
        P("seq", "head"),
        P("seq", "head"),
        P("head", "seq"),
        P("head", "seq"),
        P("seq", None),
        P("seq", None),
        P("head"),
        P("head"),
        P("head", None),
        P("head", "seq"),
        P("seq"),
        P("seq"),
    )
    return jax.shard_map(
        body,
        mesh=mesh,
        in_specs=placed,
        out_specs=(P("head", "seq"), P("head", "seq")),
        check_vma=False,
    )
```

```python
import jax
import jax.numpy as jnp
from jax import lax
from jax.sharding import PartitionSpec as P

BLOCK = 256


EPS = 1e-05


def from_behind(value, axis, steps):
    count = lax.axis_size(axis)
    leading, last = (max(0, -steps), min(count, count - steps))
    return lax.ppermute(value, axis, [(source, source + steps) for source in range(leading, last)])


def body(
    x_in,
    z_gate,
    step_size,
    log_decay,
    b_proj,
    c_proj,
    d_skip,
    norm_weight,
    w_out,
    resid,
    masked_pos,
    owner,
):
    rows_here = x_in.shape[0]
    heads_here = step_size.shape[0]
    channels = x_in.shape[1]
    head_size = channels // heads_here
    state_size = b_proj.shape[1]
    blocks = rows_here // BLOCK
    x_all = x_in.reshape(blocks, BLOCK, heads_here, head_size)
    b_all = b_proj.reshape(blocks, BLOCK, state_size)
    c_all = c_proj.reshape(blocks, BLOCK, state_size)
    dt_all = step_size.reshape(heads_here, blocks, BLOCK)
    cum_all = jnp.cumsum(log_decay.reshape(heads_here, blocks, BLOCK), axis=-1)
    lower = jnp.arange(BLOCK)[:, None] >= jnp.arange(BLOCK)[None, :]
    gram = jnp.einsum("ctn,csn->cts", c_all, b_all, preferred_element_type=jnp.float32)
    spread = cum_all[:, :, :, None] - cum_all[:, :, None, :]
    decay = jnp.where(lower[None, None], jnp.exp(jnp.where(lower[None, None], spread, 0.0)), 0.0)
    weights = (gram[None] * decay * dt_all[:, :, None, :]).astype(jnp.bfloat16)
    inner = jnp.einsum("hcts,cshp->cthp", weights, x_all, preferred_element_type=jnp.float32)
    end_weight = jnp.exp(cum_all[:, :, -1:] - cum_all) * dt_all
    keyed = (end_weight[..., None] * b_all.astype(jnp.float32)[None]).astype(jnp.bfloat16)
    block_states = jnp.einsum("hcsn,cshp->chpn", keyed, x_all, preferred_element_type=jnp.float32)
    block_decay = jnp.exp(cum_all[:, :, -1])
    running = jnp.zeros((heads_here, head_size, state_size), jnp.float32)
    reach = jnp.ones((heads_here,), jnp.float32)
    starts = []
    reaches = []
    for number in range(blocks):
        starts.append(running)
        reaches.append(reach)
        running = block_decay[:, number][:, None, None] * running + block_states[number]
        reach = reach * block_decay[:, number]
    seq_count = lax.axis_size("seq")
    log_total = jnp.sum(cum_all[:, :, -1], axis=1)
    rows = heads_here * head_size

    def pack(logs, state):
        high = lax.reduce_precision(logs, exponent_bits=8, mantissa_bits=7)
        rest = logs - high
        middle = lax.reduce_precision(rest, exponent_bits=8, mantissa_bits=7)
        spare = jnp.zeros((16, state_size), jnp.float32)
        spare = spare.at[0:3, 0:heads_here].set(jnp.stack([high, middle, rest - middle]))
        return jnp.concatenate([state.reshape(rows, state_size), spare], axis=0).astype(
            jnp.bfloat16
        )

    def unpack(slab):
        wide = slab.astype(jnp.float32)
        logs = jnp.sum(wide[rows : rows + 3, :heads_here], axis=0)
        return logs, wide[:rows].reshape(heads_here, head_size, state_size)

    logs, state = unpack(from_behind(pack(log_total, running), "seq", 1))
    distance = 1
    while distance < seq_count:
        earlier_logs, earlier_state = unpack(from_behind(pack(logs, state), "seq", distance))
        state = jnp.exp(logs)[:, None, None] * earlier_state + state
        logs = logs + earlier_logs
        distance *= 2
    incoming = state
    start_states = jnp.stack(starts) + jnp.stack(reaches)[:, :, None, None] * incoming[None]
    carried = jnp.einsum(
        "ctn,chpn->cthp",
        c_all.astype(jnp.float32),
        start_states,
        precision=lax.Precision.HIGHEST,
        preferred_element_type=jnp.float32,
    )
    carried = carried * jnp.transpose(jnp.exp(cum_all), (1, 2, 0))[:, :, :, None]
    mixed = inner + carried + d_skip[None, None, :, None] * x_all.astype(jnp.float32)
    mixed = mixed.reshape(rows_here, channels)
    gated = mixed * jax.nn.silu(z_gate.astype(jnp.float32))
    squares = lax.psum(jnp.sum(gated * gated, axis=-1), "head")
    mean_sq = squares / (channels * lax.axis_size("head"))
    hidden = (gated * norm_weight[None, :]).astype(jnp.bfloat16)
    proj = lax.psum_scatter(
        jnp.einsum("kd,tk->dt", w_out, hidden, preferred_element_type=jnp.float32).astype(
            jnp.bfloat16
        ),
        "head",
        scatter_dimension=0,
        tiled=True,
    ).astype(jnp.float32)
    proj = proj * lax.rsqrt(mean_sq + EPS)[None, :]
    block_out = (resid.astype(jnp.float32) + proj).astype(jnp.bfloat16)
    features = resid.shape[0] * lax.axis_size("head")
    masked_here = masked_pos.shape[0]
    slot_cap = 2 * masked_here // seq_count
    local_pos = masked_pos % rows_here
    owner_hot = (owner[:, None] == jnp.arange(seq_count, dtype=jnp.int32)[None, :]).astype(
        jnp.bfloat16
    )
    strictly = (jnp.arange(masked_here)[:, None] > jnp.arange(masked_here)[None, :]).astype(
        jnp.bfloat16
    )
    earlier = jnp.dot(strictly, owner_hot, preferred_element_type=jnp.float32)
    ranks = jnp.sum(earlier * owner_hot.astype(jnp.float32), axis=-1).astype(jnp.int32)
    placed = owner * slot_cap + ranks
    local_feat = resid.shape[0]
    out_wide = block_out.astype(jnp.float32)
    totals = lax.psum((jnp.sum(out_wide, axis=0), jnp.sum(out_wide * out_wide, axis=0)), "head")
    mean_col = totals[0] / features
    variance = totals[1] / features - mean_col * mean_col
    normed = ((out_wide - mean_col[None, :]) * lax.rsqrt(variance + EPS)[None, :]).astype(
        jnp.bfloat16
    )
    buffer = (
        jnp.zeros((local_feat, seq_count * slot_cap), jnp.bfloat16)
        .at[:, placed]
        .set(normed[:, local_pos])
    )
    received = lax.all_to_all(
        buffer.reshape(local_feat, seq_count, slot_cap),
        "seq",
        split_axis=1,
        concat_axis=1,
        tiled=True,
    )
    targets = received.reshape(local_feat, seq_count * slot_cap)
    return (block_out, targets)


def solution(mesh):
    placed = (
        P("seq", "head"),
        P("seq", "head"),
        P("head", "seq"),
        P("head", "seq"),
        P("seq", None),
        P("seq", None),
        P("head"),
        P("head"),
        P("head", None),
        P("head", "seq"),
        P("seq"),
        P("seq"),
    )
    return jax.shard_map(
        body,
        mesh=mesh,
        in_specs=placed,
        out_specs=(P("head", "seq"), P("head", "seq")),
        check_vma=False,
    )
```

```python
import jax
import jax.numpy as jnp
from jax import lax
from jax.sharding import PartitionSpec as P

BLOCK = 256


EPS = 1e-05


def from_behind(value, axis, steps):
    count = lax.axis_size(axis)
    leading, last = (max(0, -steps), min(count, count - steps))
    return lax.ppermute(value, axis, [(source, source + steps) for source in range(leading, last)])


def body(
    x_in,
    z_gate,
    step_size,
    log_decay,
    b_proj,
    c_proj,
    d_skip,
    norm_weight,
    w_out,
    resid,
    masked_pos,
    owner,
):
    rows_here = x_in.shape[0]
    heads_here = step_size.shape[0]
    channels = x_in.shape[1]
    head_size = channels // heads_here
    state_size = b_proj.shape[1]
    blocks = rows_here // BLOCK
    x_all = x_in.reshape(blocks, BLOCK, heads_here, head_size)
    b_all = b_proj.reshape(blocks, BLOCK, state_size)
    c_all = c_proj.reshape(blocks, BLOCK, state_size)
    dt_all = step_size.reshape(heads_here, blocks, BLOCK)
    cum_all = jnp.cumsum(log_decay.reshape(heads_here, blocks, BLOCK), axis=-1)
    lower = jnp.arange(BLOCK)[:, None] >= jnp.arange(BLOCK)[None, :]
    gram = jnp.einsum("ctn,csn->cts", c_all, b_all, preferred_element_type=jnp.float32)
    spread = cum_all[:, :, :, None] - cum_all[:, :, None, :]
    decay = jnp.where(lower[None, None], jnp.exp(jnp.where(lower[None, None], spread, 0.0)), 0.0)
    weights = (gram[None] * decay * dt_all[:, :, None, :]).astype(jnp.bfloat16)
    inner = jnp.einsum("hcts,cshp->cthp", weights, x_all, preferred_element_type=jnp.float32)
    end_weight = jnp.exp(cum_all[:, :, -1:] - cum_all) * dt_all
    keyed = (end_weight[..., None] * b_all.astype(jnp.float32)[None]).astype(jnp.bfloat16)
    block_states = jnp.einsum("hcsn,cshp->chpn", keyed, x_all, preferred_element_type=jnp.float32)
    block_decay = jnp.exp(cum_all[:, :, -1])
    running = jnp.zeros((heads_here, head_size, state_size), jnp.float32)
    reach = jnp.ones((heads_here,), jnp.float32)
    starts = []
    reaches = []
    for number in range(blocks):
        starts.append(running)
        reaches.append(reach)
        running = block_decay[:, number][:, None, None] * running + block_states[number]
        reach = reach * block_decay[:, number]
    seq_count = lax.axis_size("seq")
    log_total = jnp.sum(cum_all[:, :, -1], axis=1)
    rows = heads_here * head_size

    def pack(logs, state):
        high = lax.reduce_precision(logs, exponent_bits=8, mantissa_bits=7)
        rest = logs - high
        middle = lax.reduce_precision(rest, exponent_bits=8, mantissa_bits=7)
        spare = jnp.zeros((16, state_size), jnp.float32)
        spare = spare.at[0:3, 0:heads_here].set(jnp.stack([high, middle, rest - middle]))
        return jnp.concatenate([state.reshape(rows, state_size), spare], axis=0).astype(
            jnp.bfloat16
        )

    def unpack(slab):
        wide = slab.astype(jnp.float32)
        logs = jnp.sum(wide[rows : rows + 3, :heads_here], axis=0)
        return logs, wide[:rows].reshape(heads_here, head_size, state_size)

    logs, state = unpack(from_behind(pack(log_total, running), "seq", 1))
    distance = 1
    while distance < seq_count:
        earlier_logs, earlier_state = unpack(from_behind(pack(logs, state), "seq", distance))
        state = jnp.exp(logs)[:, None, None] * earlier_state + state
        logs = logs + earlier_logs
        distance *= 2
    incoming = state
    start_states = jnp.stack(starts) + jnp.stack(reaches)[:, :, None, None] * incoming[None]
    carried = jnp.einsum(
        "ctn,chpn->cthp",
        c_all.astype(jnp.float32),
        start_states,
        precision=lax.Precision.HIGHEST,
        preferred_element_type=jnp.float32,
    )
    carried = carried * jnp.transpose(jnp.exp(cum_all), (1, 2, 0))[:, :, :, None]
    mixed = inner + carried + d_skip[None, None, :, None] * x_all.astype(jnp.float32)
    mixed = mixed.reshape(rows_here, channels)
    gated = mixed * jax.nn.silu(z_gate.astype(jnp.float32))
    squares = lax.psum(jnp.sum(gated * gated, axis=-1), "head")
    mean_sq = squares / (channels * lax.axis_size("head"))
    hidden = (gated * norm_weight[None, :]).astype(jnp.bfloat16)
    partials = jnp.einsum("kd,tk->dt", w_out, hidden, preferred_element_type=jnp.float32).astype(
        jnp.bfloat16
    )
    groups = lax.axis_size("head")
    arrived = lax.all_to_all(
        partials.reshape(groups, partials.shape[0] // groups, rows_here),
        "head",
        0,
        0,
        tiled=False,
    )
    proj = jnp.sum(arrived.astype(jnp.float32), axis=0)
    proj = proj * lax.rsqrt(mean_sq + EPS)[None, :]
    block_out = (resid.astype(jnp.float32) + proj).astype(jnp.bfloat16)
    features = resid.shape[0] * lax.axis_size("head")
    masked_here = masked_pos.shape[0]
    slot_cap = 2 * masked_here // seq_count
    local_pos = masked_pos % rows_here
    owner_hot = (owner[:, None] == jnp.arange(seq_count, dtype=jnp.int32)[None, :]).astype(
        jnp.bfloat16
    )
    strictly = (jnp.arange(masked_here)[:, None] > jnp.arange(masked_here)[None, :]).astype(
        jnp.bfloat16
    )
    earlier = jnp.dot(strictly, owner_hot, preferred_element_type=jnp.float32)
    ranks = jnp.sum(earlier * owner_hot.astype(jnp.float32), axis=-1).astype(jnp.int32)
    placed = owner * slot_cap + ranks
    local_feat = resid.shape[0]
    out_wide = block_out.astype(jnp.float32)
    totals = lax.psum((jnp.sum(out_wide, axis=0), jnp.sum(out_wide * out_wide, axis=0)), "head")
    mean_col = totals[0] / features
    variance = totals[1] / features - mean_col * mean_col
    normed = ((out_wide - mean_col[None, :]) * lax.rsqrt(variance + EPS)[None, :]).astype(
        jnp.bfloat16
    )
    buffer = (
        jnp.zeros((local_feat, seq_count * slot_cap), jnp.bfloat16)
        .at[:, placed]
        .set(normed[:, local_pos])
    )
    received = lax.all_to_all(
        buffer.reshape(local_feat, seq_count, slot_cap),
        "seq",
        split_axis=1,
        concat_axis=1,
        tiled=True,
    )
    targets = received.reshape(local_feat, seq_count * slot_cap)
    return (block_out, targets)


def solution(mesh):
    placed = (
        P("seq", "head"),
        P("seq", "head"),
        P("head", "seq"),
        P("head", "seq"),
        P("seq", None),
        P("seq", None),
        P("head"),
        P("head"),
        P("head", None),
        P("head", "seq"),
        P("seq"),
        P("seq"),
    )
    return jax.shard_map(
        body,
        mesh=mesh,
        in_specs=placed,
        out_specs=(P("head", "seq"), P("head", "seq")),
        check_vma=False,
    )
```

```python
import jax
import jax.numpy as jnp
from jax import lax
from jax.sharding import PartitionSpec as P

BLOCK = 256


EPS = 1e-05


def from_behind(value, axis, steps):
    count = lax.axis_size(axis)
    leading, last = (max(0, -steps), min(count, count - steps))
    return lax.ppermute(value, axis, [(source, source + steps) for source in range(leading, last)])


def body(
    x_in,
    z_gate,
    step_size,
    log_decay,
    b_proj,
    c_proj,
    d_skip,
    norm_weight,
    w_out,
    resid,
    masked_pos,
    owner,
):
    rows_here = x_in.shape[0]
    heads_here = step_size.shape[0]
    channels = x_in.shape[1]
    head_size = channels // heads_here
    state_size = b_proj.shape[1]
    blocks = rows_here // BLOCK
    x_all = x_in.reshape(blocks, BLOCK, heads_here, head_size)
    b_all = b_proj.reshape(blocks, BLOCK, state_size)
    c_all = c_proj.reshape(blocks, BLOCK, state_size)
    dt_all = step_size.reshape(heads_here, blocks, BLOCK)
    cum_all = jnp.cumsum(log_decay.reshape(heads_here, blocks, BLOCK), axis=-1)
    lower = jnp.arange(BLOCK)[:, None] >= jnp.arange(BLOCK)[None, :]
    gram = jnp.einsum("ctn,csn->cts", c_all, b_all, preferred_element_type=jnp.float32)
    spread = cum_all[:, :, :, None] - cum_all[:, :, None, :]
    decay = jnp.where(lower[None, None], jnp.exp(jnp.where(lower[None, None], spread, 0.0)), 0.0)
    weights = (gram[None] * decay * dt_all[:, :, None, :]).astype(jnp.bfloat16)
    inner = jnp.einsum("hcts,cshp->cthp", weights, x_all, preferred_element_type=jnp.float32)
    end_weight = jnp.exp(cum_all[:, :, -1:] - cum_all) * dt_all
    keyed = (end_weight[..., None] * b_all.astype(jnp.float32)[None]).astype(jnp.bfloat16)
    block_states = jnp.einsum("hcsn,cshp->chpn", keyed, x_all, preferred_element_type=jnp.float32)
    block_decay = jnp.exp(cum_all[:, :, -1])
    running = jnp.zeros((heads_here, head_size, state_size), jnp.float32)
    reach = jnp.ones((heads_here,), jnp.float32)
    starts = []
    reaches = []
    for number in range(blocks):
        starts.append(running)
        reaches.append(reach)
        running = block_decay[:, number][:, None, None] * running + block_states[number]
        reach = reach * block_decay[:, number]
    seq_count = lax.axis_size("seq")
    log_total = jnp.sum(cum_all[:, :, -1], axis=1)
    rows = heads_here * head_size

    def pack(logs, state):
        high = lax.reduce_precision(logs, exponent_bits=8, mantissa_bits=7)
        rest = logs - high
        middle = lax.reduce_precision(rest, exponent_bits=8, mantissa_bits=7)
        spare = jnp.zeros((16, state_size), jnp.float32)
        spare = spare.at[0:3, 0:heads_here].set(jnp.stack([high, middle, rest - middle]))
        return jnp.concatenate([state.reshape(rows, state_size), spare], axis=0).astype(
            jnp.bfloat16
        )

    def unpack(slab):
        wide = slab.astype(jnp.float32)
        logs = jnp.sum(wide[rows : rows + 3, :heads_here], axis=0)
        return logs, wide[:rows].reshape(heads_here, head_size, state_size)

    logs, state = unpack(from_behind(pack(log_total, running), "seq", 1))
    distance = 1
    while distance < seq_count:
        earlier_logs, earlier_state = unpack(from_behind(pack(logs, state), "seq", distance))
        state = jnp.exp(logs)[:, None, None] * earlier_state + state
        logs = logs + earlier_logs
        distance *= 2
    incoming = state
    start_states = jnp.stack(starts) + jnp.stack(reaches)[:, :, None, None] * incoming[None]
    carried = jnp.einsum(
        "ctn,chpn->cthp",
        c_all.astype(jnp.float32),
        start_states,
        precision=lax.Precision.HIGHEST,
        preferred_element_type=jnp.float32,
    )
    carried = carried * jnp.transpose(jnp.exp(cum_all), (1, 2, 0))[:, :, :, None]
    mixed = inner + carried + d_skip[None, None, :, None] * x_all.astype(jnp.float32)
    mixed = mixed.reshape(rows_here, channels)
    gated = mixed * jax.nn.silu(z_gate.astype(jnp.float32))
    local_squares = jnp.sum(gated * gated, axis=-1)
    hidden = (gated * norm_weight[None, :]).astype(jnp.bfloat16)
    partials = jnp.einsum("kd,tk->dt", w_out, hidden, preferred_element_type=jnp.float32).astype(
        jnp.bfloat16
    )
    groups = lax.axis_size("head")
    high = lax.reduce_precision(local_squares, exponent_bits=8, mantissa_bits=7)
    rest = local_squares - high
    middle = lax.reduce_precision(rest, exponent_bits=8, mantissa_bits=7)
    extra = jnp.zeros((16, rows_here), jnp.float32).at[0:3].set(
        jnp.stack([high, middle, rest - middle])
    )
    extra = jnp.broadcast_to(extra.astype(jnp.bfloat16)[None], (groups, 16, rows_here))
    sent = jnp.concatenate(
        [partials.reshape(groups, partials.shape[0] // groups, rows_here), extra], axis=1
    )
    arrived = lax.all_to_all(sent, "head", 0, 0, tiled=False)
    block_rows = partials.shape[0] // groups
    proj = jnp.sum(arrived[:, :block_rows].astype(jnp.float32), axis=0)
    squares = jnp.sum(arrived[:, block_rows : block_rows + 3].astype(jnp.float32), axis=(0, 1))
    mean_sq = squares / (channels * groups)
    proj = proj * lax.rsqrt(mean_sq + EPS)[None, :]
    block_out = (resid.astype(jnp.float32) + proj).astype(jnp.bfloat16)
    features = resid.shape[0] * lax.axis_size("head")
    masked_here = masked_pos.shape[0]
    slot_cap = 2 * masked_here // seq_count
    local_pos = masked_pos % rows_here
    owner_hot = (owner[:, None] == jnp.arange(seq_count, dtype=jnp.int32)[None, :]).astype(
        jnp.bfloat16
    )
    strictly = (jnp.arange(masked_here)[:, None] > jnp.arange(masked_here)[None, :]).astype(
        jnp.bfloat16
    )
    earlier = jnp.dot(strictly, owner_hot, preferred_element_type=jnp.float32)
    ranks = jnp.sum(earlier * owner_hot.astype(jnp.float32), axis=-1).astype(jnp.int32)
    placed = owner * slot_cap + ranks
    local_feat = resid.shape[0]
    out_wide = block_out.astype(jnp.float32)
    totals = lax.psum((jnp.sum(out_wide, axis=0), jnp.sum(out_wide * out_wide, axis=0)), "head")
    mean_col = totals[0] / features
    variance = totals[1] / features - mean_col * mean_col
    normed = ((out_wide - mean_col[None, :]) * lax.rsqrt(variance + EPS)[None, :]).astype(
        jnp.bfloat16
    )
    buffer = (
        jnp.zeros((local_feat, seq_count * slot_cap), jnp.bfloat16)
        .at[:, placed]
        .set(normed[:, local_pos])
    )
    received = lax.all_to_all(
        buffer.reshape(local_feat, seq_count, slot_cap),
        "seq",
        split_axis=1,
        concat_axis=1,
        tiled=True,
    )
    targets = received.reshape(local_feat, seq_count * slot_cap)
    return (block_out, targets)


def solution(mesh):
    placed = (
        P("seq", "head"),
        P("seq", "head"),
        P("head", "seq"),
        P("head", "seq"),
        P("seq", None),
        P("seq", None),
        P("head"),
        P("head"),
        P("head", None),
        P("head", "seq"),
        P("seq"),
        P("seq"),
    )
    return jax.shard_map(
        body,
        mesh=mesh,
        in_specs=placed,
        out_specs=(P("head", "seq"), P("head", "seq")),
        check_vma=False,
    )
```

```python
import jax
import jax.numpy as jnp
from jax import lax
from jax.sharding import PartitionSpec as P

BLOCK = 256


EPS = 1e-05


def from_behind(value, axis, steps):
    count = lax.axis_size(axis)
    leading, last = (max(0, -steps), min(count, count - steps))
    return lax.ppermute(value, axis, [(source, source + steps) for source in range(leading, last)])


def body(
    x_in,
    z_gate,
    step_size,
    log_decay,
    b_proj,
    c_proj,
    d_skip,
    norm_weight,
    w_out,
    resid,
    masked_pos,
    owner,
):
    rows_here = x_in.shape[0]
    heads_here = step_size.shape[0]
    channels = x_in.shape[1]
    head_size = channels // heads_here
    state_size = b_proj.shape[1]
    blocks = rows_here // BLOCK
    x_all = x_in.reshape(blocks, BLOCK, heads_here, head_size)
    b_all = b_proj.reshape(blocks, BLOCK, state_size)
    c_all = c_proj.reshape(blocks, BLOCK, state_size)
    dt_all = step_size.reshape(heads_here, blocks, BLOCK)
    cum_all = jnp.cumsum(log_decay.reshape(heads_here, blocks, BLOCK), axis=-1)
    lower = jnp.arange(BLOCK)[:, None] >= jnp.arange(BLOCK)[None, :]
    gram = jnp.einsum("ctn,csn->cts", c_all, b_all, preferred_element_type=jnp.float32)
    spread = cum_all[:, :, :, None] - cum_all[:, :, None, :]
    decay = jnp.where(lower[None, None], jnp.exp(jnp.where(lower[None, None], spread, 0.0)), 0.0)
    weights = (gram[None] * decay * dt_all[:, :, None, :]).astype(jnp.bfloat16)
    inner = jnp.einsum("hcts,cshp->cthp", weights, x_all, preferred_element_type=jnp.float32)
    end_weight = jnp.exp(cum_all[:, :, -1:] - cum_all) * dt_all
    keyed = (end_weight[..., None] * b_all.astype(jnp.float32)[None]).astype(jnp.bfloat16)
    block_states = jnp.einsum("hcsn,cshp->chpn", keyed, x_all, preferred_element_type=jnp.float32)
    block_decay = jnp.exp(cum_all[:, :, -1])
    running = jnp.zeros((heads_here, head_size, state_size), jnp.float32)
    reach = jnp.ones((heads_here,), jnp.float32)
    starts = []
    reaches = []
    for number in range(blocks):
        starts.append(running)
        reaches.append(reach)
        running = block_decay[:, number][:, None, None] * running + block_states[number]
        reach = reach * block_decay[:, number]
    seq_count = lax.axis_size("seq")
    log_total = jnp.sum(cum_all[:, :, -1], axis=1)
    rows = heads_here * head_size

    def pack(logs, state):
        high = lax.reduce_precision(logs, exponent_bits=8, mantissa_bits=7)
        rest = logs - high
        middle = lax.reduce_precision(rest, exponent_bits=8, mantissa_bits=7)
        spare = jnp.zeros((16, state_size), jnp.float32)
        spare = spare.at[0:3, 0:heads_here].set(jnp.stack([high, middle, rest - middle]))
        return jnp.concatenate([state.reshape(rows, state_size), spare], axis=0).astype(
            jnp.bfloat16
        )

    def unpack(slab):
        wide = slab.astype(jnp.float32)
        logs = jnp.sum(wide[rows : rows + 3, :heads_here], axis=0)
        return logs, wide[:rows].reshape(heads_here, head_size, state_size)

    logs = jnp.zeros_like(log_total)
    state = jnp.zeros_like(running)
    window_logs, window_state = log_total, running
    distance = 1
    while distance < seq_count:
        earlier_logs, earlier_state = unpack(
            from_behind(pack(window_logs, window_state), "seq", distance)
        )
        state = jnp.exp(logs)[:, None, None] * earlier_state + state
        logs = logs + earlier_logs
        distance *= 2
        if distance < seq_count:
            window_state = jnp.exp(log_total)[:, None, None] * state + running
            window_logs = logs + log_total
    incoming = state
    start_states = jnp.stack(starts) + jnp.stack(reaches)[:, :, None, None] * incoming[None]
    carried = jnp.einsum(
        "ctn,chpn->cthp",
        c_all.astype(jnp.float32),
        start_states,
        precision=lax.Precision.HIGHEST,
        preferred_element_type=jnp.float32,
    )
    carried = carried * jnp.transpose(jnp.exp(cum_all), (1, 2, 0))[:, :, :, None]
    mixed = inner + carried + d_skip[None, None, :, None] * x_all.astype(jnp.float32)
    mixed = mixed.reshape(rows_here, channels)
    gated = mixed * jax.nn.silu(z_gate.astype(jnp.float32))
    local_squares = jnp.sum(gated * gated, axis=-1)
    hidden = (gated * norm_weight[None, :]).astype(jnp.bfloat16)
    partials = jnp.einsum("kd,tk->dt", w_out, hidden, preferred_element_type=jnp.float32).astype(
        jnp.bfloat16
    )
    groups = lax.axis_size("head")
    high = lax.reduce_precision(local_squares, exponent_bits=8, mantissa_bits=7)
    rest = local_squares - high
    middle = lax.reduce_precision(rest, exponent_bits=8, mantissa_bits=7)
    extra = jnp.zeros((16, rows_here), jnp.float32).at[0:3].set(
        jnp.stack([high, middle, rest - middle])
    )
    extra = jnp.broadcast_to(extra.astype(jnp.bfloat16)[None], (groups, 16, rows_here))
    sent = jnp.concatenate(
        [partials.reshape(groups, partials.shape[0] // groups, rows_here), extra], axis=1
    )
    arrived = lax.all_to_all(sent, "head", 0, 0, tiled=False)
    block_rows = partials.shape[0] // groups
    proj = jnp.sum(arrived[:, :block_rows].astype(jnp.float32), axis=0)
    squares = jnp.sum(arrived[:, block_rows : block_rows + 3].astype(jnp.float32), axis=(0, 1))
    mean_sq = squares / (channels * groups)
    proj = proj * lax.rsqrt(mean_sq + EPS)[None, :]
    block_out = (resid.astype(jnp.float32) + proj).astype(jnp.bfloat16)
    features = resid.shape[0] * lax.axis_size("head")
    masked_here = masked_pos.shape[0]
    slot_cap = 2 * masked_here // seq_count
    local_pos = masked_pos % rows_here
    owner_hot = (owner[:, None] == jnp.arange(seq_count, dtype=jnp.int32)[None, :]).astype(
        jnp.bfloat16
    )
    strictly = (jnp.arange(masked_here)[:, None] > jnp.arange(masked_here)[None, :]).astype(
        jnp.bfloat16
    )
    earlier = jnp.dot(strictly, owner_hot, preferred_element_type=jnp.float32)
    ranks = jnp.sum(earlier * owner_hot.astype(jnp.float32), axis=-1).astype(jnp.int32)
    placed = owner * slot_cap + ranks
    local_feat = resid.shape[0]
    out_wide = block_out.astype(jnp.float32)
    totals = lax.psum((jnp.sum(out_wide, axis=0), jnp.sum(out_wide * out_wide, axis=0)), "head")
    mean_col = totals[0] / features
    variance = totals[1] / features - mean_col * mean_col
    normed = ((out_wide - mean_col[None, :]) * lax.rsqrt(variance + EPS)[None, :]).astype(
        jnp.bfloat16
    )
    buffer = (
        jnp.zeros((local_feat, seq_count * slot_cap), jnp.bfloat16)
        .at[:, placed]
        .set(normed[:, local_pos])
    )
    received = lax.all_to_all(
        buffer.reshape(local_feat, seq_count, slot_cap),
        "seq",
        split_axis=1,
        concat_axis=1,
        tiled=True,
    )
    targets = received.reshape(local_feat, seq_count * slot_cap)
    return (block_out, targets)


def solution(mesh):
    placed = (
        P("seq", "head"),
        P("seq", "head"),
        P("head", "seq"),
        P("head", "seq"),
        P("seq", None),
        P("seq", None),
        P("head"),
        P("head"),
        P("head", None),
        P("head", "seq"),
        P("seq"),
        P("seq"),
    )
    return jax.shard_map(
        body,
        mesh=mesh,
        in_specs=placed,
        out_specs=(P("head", "seq"), P("head", "seq")),
        check_vma=False,
    )
```

```python
import jax
import jax.numpy as jnp
from jax import lax
from jax.sharding import PartitionSpec as P

BLOCK = 256


EPS = 1e-05


def from_behind(value, axis, steps):
    count = lax.axis_size(axis)
    leading, last = (max(0, -steps), min(count, count - steps))
    return lax.ppermute(value, axis, [(source, source + steps) for source in range(leading, last)])


def body(
    x_in,
    z_gate,
    step_size,
    log_decay,
    b_proj,
    c_proj,
    d_skip,
    norm_weight,
    w_out,
    resid,
    masked_pos,
    owner,
):
    rows_here = x_in.shape[0]
    heads_here = step_size.shape[0]
    channels = x_in.shape[1]
    head_size = channels // heads_here
    state_size = b_proj.shape[1]
    blocks = rows_here // BLOCK
    x_all = x_in.reshape(blocks, BLOCK, heads_here, head_size)
    b_all = b_proj.reshape(blocks, BLOCK, state_size)
    c_all = c_proj.reshape(blocks, BLOCK, state_size)
    dt_all = step_size.reshape(heads_here, blocks, BLOCK)
    cum_all = jnp.cumsum(log_decay.reshape(heads_here, blocks, BLOCK), axis=-1)
    lower = jnp.arange(BLOCK)[:, None] >= jnp.arange(BLOCK)[None, :]
    gram = jnp.einsum("ctn,csn->cts", c_all, b_all, preferred_element_type=jnp.float32)
    spread = cum_all[:, :, :, None] - cum_all[:, :, None, :]
    decay = jnp.where(lower[None, None], jnp.exp(jnp.where(lower[None, None], spread, 0.0)), 0.0)
    weights = (gram[None] * decay * dt_all[:, :, None, :]).astype(jnp.bfloat16)
    inner = jnp.einsum("hcts,cshp->cthp", weights, x_all, preferred_element_type=jnp.float32)
    end_weight = jnp.exp(cum_all[:, :, -1:] - cum_all) * dt_all
    keyed = (end_weight[..., None] * b_all.astype(jnp.float32)[None]).astype(jnp.bfloat16)
    block_states = jnp.einsum("hcsn,cshp->chpn", keyed, x_all, preferred_element_type=jnp.float32)
    block_decay = jnp.exp(cum_all[:, :, -1])
    running = jnp.zeros((heads_here, head_size, state_size), jnp.float32)
    reach = jnp.ones((heads_here,), jnp.float32)
    starts = []
    reaches = []
    for number in range(blocks):
        starts.append(running)
        reaches.append(reach)
        running = block_decay[:, number][:, None, None] * running + block_states[number]
        reach = reach * block_decay[:, number]
    seq_count = lax.axis_size("seq")
    log_total = jnp.sum(cum_all[:, :, -1], axis=1)
    rows = heads_here * head_size

    def pack(logs, state):
        high = lax.reduce_precision(logs, exponent_bits=8, mantissa_bits=7)
        rest = logs - high
        middle = lax.reduce_precision(rest, exponent_bits=8, mantissa_bits=7)
        spare = jnp.zeros((16, state_size), jnp.float32)
        spare = spare.at[0:3, 0:heads_here].set(jnp.stack([high, middle, rest - middle]))
        return jnp.concatenate([state.reshape(rows, state_size), spare], axis=0).astype(
            jnp.bfloat16
        )

    def unpack(slab):
        wide = slab.astype(jnp.float32)
        logs = jnp.sum(wide[rows : rows + 3, :heads_here], axis=0)
        return logs, wide[:rows].reshape(heads_here, head_size, state_size)

    logs = jnp.zeros_like(log_total)
    state = jnp.zeros_like(running)
    window_logs, window_state = log_total, running
    distance = 1
    while distance < seq_count:
        earlier_logs, earlier_state = unpack(
            from_behind(pack(window_logs, window_state), "seq", distance)
        )
        state = jnp.exp(logs)[:, None, None] * earlier_state + state
        logs = logs + earlier_logs
        distance *= 2
        if distance < seq_count:
            window_state = jnp.exp(log_total)[:, None, None] * state + running
            window_logs = logs + log_total
    incoming = state
    start_states = jnp.stack(starts) + jnp.stack(reaches)[:, :, None, None] * incoming[None]
    carried = jnp.einsum(
        "ctn,chpn->cthp",
        c_all.astype(jnp.float32),
        start_states,
        precision=lax.Precision.HIGHEST,
        preferred_element_type=jnp.float32,
    )
    carried = carried * jnp.transpose(jnp.exp(cum_all), (1, 2, 0))[:, :, :, None]
    mixed = inner + carried + d_skip[None, None, :, None] * x_all.astype(jnp.float32)
    mixed = mixed.reshape(rows_here, channels)
    gated = mixed * jax.nn.silu(z_gate.astype(jnp.float32))
    local_squares = jnp.sum(gated * gated, axis=-1)
    hidden = (gated * norm_weight[None, :]).astype(jnp.bfloat16)
    partials = jnp.einsum("kd,tk->dt", w_out, hidden, preferred_element_type=jnp.float32).astype(
        jnp.bfloat16
    )
    groups = lax.axis_size("head")
    high = lax.reduce_precision(local_squares, exponent_bits=8, mantissa_bits=7)
    rest = local_squares - high
    middle = lax.reduce_precision(rest, exponent_bits=8, mantissa_bits=7)
    extra = jnp.zeros((16, rows_here), jnp.float32).at[0:3].set(
        jnp.stack([high, middle, rest - middle])
    )
    extra = jnp.broadcast_to(extra.astype(jnp.bfloat16)[None], (groups, 16, rows_here))
    sent = jnp.concatenate(
        [partials.reshape(groups, partials.shape[0] // groups, rows_here), extra], axis=1
    )
    arrived = lax.all_to_all(sent, "head", 0, 0, tiled=False)
    block_rows = partials.shape[0] // groups
    proj = jnp.sum(arrived[:, :block_rows].astype(jnp.float32), axis=0)
    squares = jnp.sum(arrived[:, block_rows : block_rows + 3].astype(jnp.float32), axis=(0, 1))
    mean_sq = squares / (channels * groups)
    proj = proj * lax.rsqrt(mean_sq + EPS)[None, :]
    block_out = (resid.astype(jnp.float32) + proj).astype(jnp.bfloat16)
    features = resid.shape[0] * lax.axis_size("head")
    masked_here = masked_pos.shape[0]
    slot_cap = 2 * masked_here // seq_count
    local_pos = masked_pos % rows_here
    owner_hot = (owner[:, None] == jnp.arange(seq_count, dtype=jnp.int32)[None, :]).astype(
        jnp.bfloat16
    )
    strictly = (jnp.arange(masked_here)[:, None] > jnp.arange(masked_here)[None, :]).astype(
        jnp.bfloat16
    )
    earlier = jnp.dot(strictly, owner_hot, preferred_element_type=jnp.float32)
    ranks = jnp.sum(earlier * owner_hot.astype(jnp.float32), axis=-1).astype(jnp.int32)
    placed = owner * slot_cap + ranks
    local_feat = resid.shape[0]
    out_wide = block_out.astype(jnp.float32)
    totals = lax.psum((jnp.sum(out_wide, axis=0), jnp.sum(out_wide * out_wide, axis=0)), "head")
    mean_col = totals[0] / features
    variance = totals[1] / features - mean_col * mean_col
    normed = ((out_wide - mean_col[None, :]) * lax.rsqrt(variance + EPS)[None, :]).astype(
        jnp.bfloat16
    )
    pos_hot = (local_pos[:, None] == jnp.arange(rows_here)[None, :]).astype(jnp.bfloat16)
    slot_hot = (placed[:, None] == jnp.arange(seq_count * slot_cap)[None, :]).astype(jnp.bfloat16)
    select = jnp.einsum("jp,js->ps", pos_hot, slot_hot, preferred_element_type=jnp.float32)
    buffer = jnp.dot(
        normed, select.astype(jnp.bfloat16), preferred_element_type=jnp.float32
    ).astype(jnp.bfloat16)
    received = lax.all_to_all(
        buffer.reshape(local_feat, seq_count, slot_cap),
        "seq",
        split_axis=1,
        concat_axis=1,
        tiled=True,
    )
    targets = received.reshape(local_feat, seq_count * slot_cap)
    return (block_out, targets)


def solution(mesh):
    placed = (
        P("seq", "head"),
        P("seq", "head"),
        P("head", "seq"),
        P("head", "seq"),
        P("seq", None),
        P("seq", None),
        P("head"),
        P("head"),
        P("head", None),
        P("head", "seq"),
        P("seq"),
        P("seq"),
    )
    return jax.shard_map(
        body,
        mesh=mesh,
        in_specs=placed,
        out_specs=(P("head", "seq"), P("head", "seq")),
        check_vma=False,
    )
```

```python
import jax
import jax.numpy as jnp
from jax import lax
from jax.sharding import PartitionSpec as P

BLOCK = 256


EPS = 1e-05


def from_behind(value, axis, steps):
    count = lax.axis_size(axis)
    leading, last = (max(0, -steps), min(count, count - steps))
    return lax.ppermute(value, axis, [(source, source + steps) for source in range(leading, last)])


def body(
    x_in,
    z_gate,
    step_size,
    log_decay,
    b_proj,
    c_proj,
    d_skip,
    norm_weight,
    w_out,
    resid,
    masked_pos,
    owner,
):
    rows_here = x_in.shape[0]
    heads_here = step_size.shape[0]
    channels = x_in.shape[1]
    head_size = channels // heads_here
    state_size = b_proj.shape[1]
    blocks = rows_here // BLOCK
    x_all = x_in.reshape(blocks, BLOCK, heads_here, head_size)
    b_all = b_proj.reshape(blocks, BLOCK, state_size)
    c_all = c_proj.reshape(blocks, BLOCK, state_size)
    dt_all = step_size.reshape(heads_here, blocks, BLOCK)
    cum_all = jnp.cumsum(log_decay.reshape(heads_here, blocks, BLOCK), axis=-1)
    lower = jnp.arange(BLOCK)[:, None] >= jnp.arange(BLOCK)[None, :]
    gram = jnp.einsum("ctn,csn->cts", c_all, b_all, preferred_element_type=jnp.float32)
    spread = cum_all[:, :, :, None] - cum_all[:, :, None, :]
    decay = jnp.where(lower[None, None], jnp.exp(jnp.where(lower[None, None], spread, 0.0)), 0.0)
    weights = (gram[None] * decay * dt_all[:, :, None, :]).astype(jnp.bfloat16)
    inner = jnp.einsum("hcts,cshp->cthp", weights, x_all, preferred_element_type=jnp.float32)
    end_weight = jnp.exp(cum_all[:, :, -1:] - cum_all) * dt_all
    keyed = (end_weight[..., None] * b_all.astype(jnp.float32)[None]).astype(jnp.bfloat16)
    block_states = jnp.einsum("hcsn,cshp->chpn", keyed, x_all, preferred_element_type=jnp.float32)
    block_decay = jnp.exp(cum_all[:, :, -1])
    running = jnp.zeros((heads_here, head_size, state_size), jnp.float32)
    reach = jnp.ones((heads_here,), jnp.float32)
    starts = []
    reaches = []
    for number in range(blocks):
        starts.append(running)
        reaches.append(reach)
        running = block_decay[:, number][:, None, None] * running + block_states[number]
        reach = reach * block_decay[:, number]
    seq_count = lax.axis_size("seq")
    log_total = jnp.sum(cum_all[:, :, -1], axis=1)
    rows = heads_here * head_size

    def pack(logs, state):
        high = lax.reduce_precision(logs, exponent_bits=8, mantissa_bits=7)
        rest = logs - high
        middle = lax.reduce_precision(rest, exponent_bits=8, mantissa_bits=7)
        spare = jnp.zeros((16, state_size), jnp.float32)
        spare = spare.at[0:3, 0:heads_here].set(jnp.stack([high, middle, rest - middle]))
        return jnp.concatenate([state.reshape(rows, state_size), spare], axis=0).astype(
            jnp.bfloat16
        )

    def unpack(slab):
        wide = slab.astype(jnp.float32)
        logs = jnp.sum(wide[rows : rows + 3, :heads_here], axis=0)
        return logs, wide[:rows].reshape(heads_here, head_size, state_size)

    logs = jnp.zeros_like(log_total)
    state = jnp.zeros_like(running)
    window_logs, window_state = log_total, running
    distance = 1
    while distance < seq_count:
        earlier_logs, earlier_state = unpack(
            from_behind(pack(window_logs, window_state), "seq", distance)
        )
        state = jnp.exp(logs)[:, None, None] * earlier_state + state
        logs = logs + earlier_logs
        distance *= 2
        if distance < seq_count:
            window_state = jnp.exp(log_total)[:, None, None] * state + running
            window_logs = logs + log_total
    incoming = state
    start_states = jnp.stack(starts) + jnp.stack(reaches)[:, :, None, None] * incoming[None]
    carried = jnp.einsum(
        "ctn,chpn->cthp",
        c_all.astype(jnp.float32),
        start_states,
        precision=lax.Precision.HIGHEST,
        preferred_element_type=jnp.float32,
    )
    carried = carried * jnp.transpose(jnp.exp(cum_all), (1, 2, 0))[:, :, :, None]
    mixed = inner + carried + d_skip[None, None, :, None] * x_all.astype(jnp.float32)
    mixed = mixed.reshape(rows_here, channels)
    gated = mixed * jax.nn.silu(z_gate.astype(jnp.float32))
    local_squares = jnp.sum(gated * gated, axis=-1)
    hidden = (gated * norm_weight[None, :]).astype(jnp.bfloat16)
    groups = lax.axis_size("head")
    block_rows = w_out.shape[1] // groups
    padded_w = jnp.pad(
        jnp.transpose(w_out.reshape(w_out.shape[0], groups, block_rows), (1, 2, 0)),
        ((0, 0), (0, 16), (0, 0)),
    )
    high = lax.reduce_precision(local_squares, exponent_bits=8, mantissa_bits=7)
    rest = local_squares - high
    middle = lax.reduce_precision(rest, exponent_bits=8, mantissa_bits=7)
    extra = jnp.zeros((block_rows + 16, rows_here), jnp.float32).at[block_rows : block_rows + 3].set(
        jnp.stack([high, middle, rest - middle])
    )
    sent = (
        jnp.einsum("gdk,tk->gdt", padded_w, hidden, preferred_element_type=jnp.float32).astype(
            jnp.bfloat16
        )
        + extra.astype(jnp.bfloat16)[None]
    )
    arrived = lax.all_to_all(sent, "head", 0, 0, tiled=False)
    proj = jnp.sum(arrived[:, :block_rows].astype(jnp.float32), axis=0)
    squares = jnp.sum(arrived[:, block_rows : block_rows + 3].astype(jnp.float32), axis=(0, 1))
    mean_sq = squares / (channels * groups)
    proj = proj * lax.rsqrt(mean_sq + EPS)[None, :]
    block_out = (resid.astype(jnp.float32) + proj).astype(jnp.bfloat16)
    features = resid.shape[0] * lax.axis_size("head")
    masked_here = masked_pos.shape[0]
    slot_cap = 2 * masked_here // seq_count
    local_pos = masked_pos % rows_here
    owner_hot = (owner[:, None] == jnp.arange(seq_count, dtype=jnp.int32)[None, :]).astype(
        jnp.bfloat16
    )
    strictly = (jnp.arange(masked_here)[:, None] > jnp.arange(masked_here)[None, :]).astype(
        jnp.bfloat16
    )
    earlier = jnp.dot(strictly, owner_hot, preferred_element_type=jnp.float32)
    ranks = jnp.sum(earlier * owner_hot.astype(jnp.float32), axis=-1).astype(jnp.int32)
    placed = owner * slot_cap + ranks
    local_feat = resid.shape[0]
    out_wide = block_out.astype(jnp.float32)
    totals = lax.psum((jnp.sum(out_wide, axis=0), jnp.sum(out_wide * out_wide, axis=0)), "head")
    mean_col = totals[0] / features
    variance = totals[1] / features - mean_col * mean_col
    normed = ((out_wide - mean_col[None, :]) * lax.rsqrt(variance + EPS)[None, :]).astype(
        jnp.bfloat16
    )
    pos_hot = (local_pos[:, None] == jnp.arange(rows_here)[None, :]).astype(jnp.bfloat16)
    slot_hot = (placed[:, None] == jnp.arange(seq_count * slot_cap)[None, :]).astype(jnp.bfloat16)
    select = jnp.einsum("jp,js->ps", pos_hot, slot_hot, preferred_element_type=jnp.float32)
    buffer = jnp.dot(
        normed, select.astype(jnp.bfloat16), preferred_element_type=jnp.float32
    ).astype(jnp.bfloat16)
    received = lax.all_to_all(
        buffer.reshape(local_feat, seq_count, slot_cap),
        "seq",
        split_axis=1,
        concat_axis=1,
        tiled=True,
    )
    targets = received.reshape(local_feat, seq_count * slot_cap)
    return (block_out, targets)


def solution(mesh):
    placed = (
        P("seq", "head"),
        P("seq", "head"),
        P("head", "seq"),
        P("head", "seq"),
        P("seq", None),
        P("seq", None),
        P("head"),
        P("head"),
        P("head", None),
        P("head", "seq"),
        P("seq"),
        P("seq"),
    )
    return jax.shard_map(
        body,
        mesh=mesh,
        in_specs=placed,
        out_specs=(P("head", "seq"), P("head", "seq")),
        check_vma=False,
    )
```

```python
import jax
import jax.numpy as jnp
from jax import lax
from jax.sharding import PartitionSpec as P

BLOCK = 256


EPS = 1e-05


def from_behind(value, axis, steps):
    count = lax.axis_size(axis)
    leading, last = (max(0, -steps), min(count, count - steps))
    return lax.ppermute(value, axis, [(source, source + steps) for source in range(leading, last)])


def body(
    x_in,
    z_gate,
    step_size,
    log_decay,
    b_proj,
    c_proj,
    d_skip,
    norm_weight,
    w_out,
    resid,
    masked_pos,
    owner,
):
    rows_here = x_in.shape[0]
    heads_here = step_size.shape[0]
    channels = x_in.shape[1]
    head_size = channels // heads_here
    state_size = b_proj.shape[1]
    blocks = rows_here // BLOCK
    x_all = x_in.reshape(blocks, BLOCK, heads_here, head_size)
    b_all = b_proj.reshape(blocks, BLOCK, state_size)
    c_all = c_proj.reshape(blocks, BLOCK, state_size)
    dt_all = step_size.reshape(heads_here, blocks, BLOCK)
    cum_all = jnp.cumsum(log_decay.reshape(heads_here, blocks, BLOCK), axis=-1)
    lower = jnp.arange(BLOCK)[:, None] >= jnp.arange(BLOCK)[None, :]
    gram = jnp.einsum("ctn,csn->cts", c_all, b_all, preferred_element_type=jnp.float32)
    spread = cum_all[:, :, :, None] - cum_all[:, :, None, :]
    decay = jnp.where(lower[None, None], jnp.exp(jnp.where(lower[None, None], spread, 0.0)), 0.0)
    weights = (gram[None] * decay * dt_all[:, :, None, :]).astype(jnp.bfloat16)
    inner = jnp.einsum("hcts,cshp->cthp", weights, x_all, preferred_element_type=jnp.float32)
    end_weight = jnp.exp(cum_all[:, :, -1:] - cum_all) * dt_all
    keyed = (end_weight[..., None] * b_all.astype(jnp.float32)[None]).astype(jnp.bfloat16)
    block_states = jnp.einsum("hcsn,cshp->chpn", keyed, x_all, preferred_element_type=jnp.float32)
    block_decay = jnp.exp(cum_all[:, :, -1])
    running = jnp.zeros((heads_here, head_size, state_size), jnp.float32)
    reach = jnp.ones((heads_here,), jnp.float32)
    starts = []
    reaches = []
    for number in range(blocks):
        starts.append(running)
        reaches.append(reach)
        running = block_decay[:, number][:, None, None] * running + block_states[number]
        reach = reach * block_decay[:, number]
    seq_count = lax.axis_size("seq")
    log_total = jnp.sum(cum_all[:, :, -1], axis=1)
    rows = heads_here * head_size

    def pack(logs, state):
        high = lax.reduce_precision(logs, exponent_bits=8, mantissa_bits=7)
        rest = logs - high
        middle = lax.reduce_precision(rest, exponent_bits=8, mantissa_bits=7)
        spare = jnp.zeros((16, state_size), jnp.float32)
        spare = spare.at[0:3, 0:heads_here].set(jnp.stack([high, middle, rest - middle]))
        return jnp.concatenate([state.reshape(rows, state_size), spare], axis=0).astype(
            jnp.bfloat16
        )

    def unpack(slab):
        wide = slab.astype(jnp.float32)
        logs = jnp.sum(wide[rows : rows + 3, :heads_here], axis=0)
        return logs, wide[:rows].reshape(heads_here, head_size, state_size)

    logs = jnp.zeros_like(log_total)
    state = jnp.zeros_like(running)
    window_logs, window_state = log_total, running
    distance = 1
    while distance < seq_count:
        earlier_logs, earlier_state = unpack(
            from_behind(pack(window_logs, window_state), "seq", distance)
        )
        state = jnp.exp(logs)[:, None, None] * earlier_state + state
        logs = logs + earlier_logs
        distance *= 2
        if distance < seq_count:
            window_state = jnp.exp(log_total)[:, None, None] * state + running
            window_logs = logs + log_total
    incoming = state
    start_states = jnp.stack(starts) + jnp.stack(reaches)[:, :, None, None] * incoming[None]
    carried = jnp.einsum(
        "ctn,chpn->cthp",
        c_all.astype(jnp.float32),
        start_states,
        precision=lax.Precision.HIGHEST,
        preferred_element_type=jnp.float32,
    )
    carried = carried * jnp.transpose(jnp.exp(cum_all), (1, 2, 0))[:, :, :, None]
    mixed = inner + carried + d_skip[None, None, :, None] * x_all.astype(jnp.float32)
    mixed = mixed.reshape(rows_here, channels)
    gated = mixed * jax.nn.silu(z_gate.astype(jnp.float32))
    local_squares = jnp.sum(gated * gated, axis=-1)
    hidden = (gated * norm_weight[None, :]).astype(jnp.bfloat16)
    groups = lax.axis_size("head")
    block_rows = w_out.shape[1] // groups
    padded_w = jnp.pad(
        jnp.transpose(w_out.reshape(w_out.shape[0], groups, block_rows), (1, 2, 0)),
        ((0, 0), (0, 16), (0, 16)),
    )
    out_row = jnp.arange(block_rows + 16)[:, None]
    in_col = jnp.arange(channels + 16)[None, :]
    marker = (out_row - block_rows == in_col - channels) & (out_row >= block_rows) & (
        out_row < block_rows + 3
    )
    padded_w = padded_w + marker.astype(jnp.bfloat16)[None]
    high = lax.reduce_precision(local_squares, exponent_bits=8, mantissa_bits=7)
    rest = local_squares - high
    middle = lax.reduce_precision(rest, exponent_bits=8, mantissa_bits=7)
    parts = jnp.zeros((rows_here, 16), jnp.float32).at[:, 0:3].set(
        jnp.stack([high, middle, rest - middle], axis=1)
    )
    widened = jnp.concatenate([hidden, parts.astype(jnp.bfloat16)], axis=1)
    sent = jnp.einsum(
        "gdk,tk->gdt", padded_w, widened, preferred_element_type=jnp.float32
    ).astype(jnp.bfloat16)
    arrived = lax.all_to_all(sent, "head", 0, 0, tiled=False)
    proj = jnp.sum(arrived[:, :block_rows].astype(jnp.float32), axis=0)
    squares = jnp.sum(arrived[:, block_rows : block_rows + 3].astype(jnp.float32), axis=(0, 1))
    mean_sq = squares / (channels * groups)
    proj = proj * lax.rsqrt(mean_sq + EPS)[None, :]
    block_out = (resid.astype(jnp.float32) + proj).astype(jnp.bfloat16)
    features = resid.shape[0] * lax.axis_size("head")
    masked_here = masked_pos.shape[0]
    slot_cap = 2 * masked_here // seq_count
    local_pos = masked_pos % rows_here
    owner_hot = (owner[:, None] == jnp.arange(seq_count, dtype=jnp.int32)[None, :]).astype(
        jnp.bfloat16
    )
    strictly = (jnp.arange(masked_here)[:, None] > jnp.arange(masked_here)[None, :]).astype(
        jnp.bfloat16
    )
    earlier = jnp.dot(strictly, owner_hot, preferred_element_type=jnp.float32)
    ranks = jnp.sum(earlier * owner_hot.astype(jnp.float32), axis=-1).astype(jnp.int32)
    placed = owner * slot_cap + ranks
    local_feat = resid.shape[0]
    out_wide = block_out.astype(jnp.float32)
    totals = lax.psum((jnp.sum(out_wide, axis=0), jnp.sum(out_wide * out_wide, axis=0)), "head")
    mean_col = totals[0] / features
    variance = totals[1] / features - mean_col * mean_col
    normed = ((out_wide - mean_col[None, :]) * lax.rsqrt(variance + EPS)[None, :]).astype(
        jnp.bfloat16
    )
    pos_hot = (local_pos[:, None] == jnp.arange(rows_here)[None, :]).astype(jnp.bfloat16)
    slot_hot = (placed[:, None] == jnp.arange(seq_count * slot_cap)[None, :]).astype(jnp.bfloat16)
    select = jnp.einsum("jp,js->ps", pos_hot, slot_hot, preferred_element_type=jnp.float32)
    buffer = jnp.dot(
        normed, select.astype(jnp.bfloat16), preferred_element_type=jnp.float32
    ).astype(jnp.bfloat16)
    received = lax.all_to_all(
        buffer.reshape(local_feat, seq_count, slot_cap),
        "seq",
        split_axis=1,
        concat_axis=1,
        tiled=True,
    )
    targets = received.reshape(local_feat, seq_count * slot_cap)
    return (block_out, targets)


def solution(mesh):
    placed = (
        P("seq", "head"),
        P("seq", "head"),
        P("head", "seq"),
        P("head", "seq"),
        P("seq", None),
        P("seq", None),
        P("head"),
        P("head"),
        P("head", None),
        P("head", "seq"),
        P("seq"),
        P("seq"),
    )
    return jax.shard_map(
        body,
        mesh=mesh,
        in_specs=placed,
        out_specs=(P("head", "seq"), P("head", "seq")),
        check_vma=False,
    )
```

```python
import jax
import jax.numpy as jnp
from jax import lax
from jax.sharding import Mesh, PartitionSpec as P

BLOCK = 256


EPS = 1e-05


def from_behind(value, axis, steps):
    count = lax.axis_size(axis)
    leading, last = (max(0, -steps), min(count, count - steps))
    return lax.ppermute(value, axis, [(source, source + steps) for source in range(leading, last)])


def body(
    x_in,
    z_gate,
    step_size,
    log_decay,
    b_proj,
    c_proj,
    d_skip,
    norm_weight,
    w_out,
    resid,
    masked_pos,
    owner,
):
    rows_here = x_in.shape[0]
    heads_here = step_size.shape[0]
    channels = x_in.shape[1]
    head_size = channels // heads_here
    state_size = b_proj.shape[1]
    blocks = rows_here // BLOCK
    x_all = x_in.reshape(blocks, BLOCK, heads_here, head_size)
    b_all = b_proj.reshape(blocks, BLOCK, state_size)
    c_all = c_proj.reshape(blocks, BLOCK, state_size)
    dt_all = step_size.reshape(heads_here, blocks, BLOCK)
    cum_all = jnp.cumsum(log_decay.reshape(heads_here, blocks, BLOCK), axis=-1)
    lower = jnp.arange(BLOCK)[:, None] >= jnp.arange(BLOCK)[None, :]
    gram = jnp.einsum("ctn,csn->cts", c_all, b_all, preferred_element_type=jnp.float32)
    spread = cum_all[:, :, :, None] - cum_all[:, :, None, :]
    decay = jnp.where(lower[None, None], jnp.exp(jnp.where(lower[None, None], spread, 0.0)), 0.0)
    weights = (gram[None] * decay * dt_all[:, :, None, :]).astype(jnp.bfloat16)
    inner = jnp.einsum("hcts,cshp->cthp", weights, x_all, preferred_element_type=jnp.float32)
    end_weight = jnp.exp(cum_all[:, :, -1:] - cum_all) * dt_all
    keyed = (end_weight[..., None] * b_all.astype(jnp.float32)[None]).astype(jnp.bfloat16)
    block_states = jnp.einsum("hcsn,cshp->chpn", keyed, x_all, preferred_element_type=jnp.float32)
    block_decay = jnp.exp(cum_all[:, :, -1])
    running = jnp.zeros((heads_here, head_size, state_size), jnp.float32)
    reach = jnp.ones((heads_here,), jnp.float32)
    starts = []
    reaches = []
    for number in range(blocks):
        starts.append(running)
        reaches.append(reach)
        running = block_decay[:, number][:, None, None] * running + block_states[number]
        reach = reach * block_decay[:, number]
    seq_count = lax.axis_size("seq")
    log_total = jnp.sum(cum_all[:, :, -1], axis=1)
    rows = heads_here * head_size

    def pack(logs, state):
        high = lax.reduce_precision(logs, exponent_bits=8, mantissa_bits=7)
        rest = logs - high
        middle = lax.reduce_precision(rest, exponent_bits=8, mantissa_bits=7)
        spare = jnp.zeros((16, state_size), jnp.float32)
        spare = spare.at[0:3, 0:heads_here].set(jnp.stack([high, middle, rest - middle]))
        return jnp.concatenate([state.reshape(rows, state_size), spare], axis=0).astype(
            jnp.bfloat16
        )

    def unpack(slab):
        wide = slab.astype(jnp.float32)
        logs = jnp.sum(wide[rows : rows + 3, :heads_here], axis=0)
        return logs, wide[:rows].reshape(heads_here, head_size, state_size)

    logs = jnp.zeros_like(log_total)
    state = jnp.zeros_like(running)
    window_logs, window_state = log_total, running
    distance = 1
    while distance < seq_count:
        earlier_logs, earlier_state = unpack(
            from_behind(pack(window_logs, window_state), "seq", distance)
        )
        state = jnp.exp(logs)[:, None, None] * earlier_state + state
        logs = logs + earlier_logs
        distance *= 2
        if distance < seq_count:
            window_state = jnp.exp(log_total)[:, None, None] * state + running
            window_logs = logs + log_total
    incoming = state
    start_states = jnp.stack(starts) + jnp.stack(reaches)[:, :, None, None] * incoming[None]
    carried = jnp.einsum(
        "ctn,chpn->cthp",
        c_all.astype(jnp.float32),
        start_states,
        precision=lax.Precision.HIGHEST,
        preferred_element_type=jnp.float32,
    )
    carried = carried * jnp.transpose(jnp.exp(cum_all), (1, 2, 0))[:, :, :, None]
    mixed = inner + carried + d_skip[None, None, :, None] * x_all.astype(jnp.float32)
    mixed = mixed.reshape(rows_here, channels)
    gated = mixed * jax.nn.silu(z_gate.astype(jnp.float32))
    local_squares = jnp.sum(gated * gated, axis=-1)
    hidden = (gated * norm_weight[None, :]).astype(jnp.bfloat16)
    groups = lax.axis_size("x") * lax.axis_size("core")
    block_rows = w_out.shape[1] // groups
    padded_w = jnp.pad(
        jnp.transpose(w_out.reshape(w_out.shape[0], groups, block_rows), (1, 2, 0)),
        ((0, 0), (0, 16), (0, 16)),
    )
    out_row = jnp.arange(block_rows + 16)[:, None]
    in_col = jnp.arange(channels + 16)[None, :]
    marker = (out_row - block_rows == in_col - channels) & (out_row >= block_rows) & (
        out_row < block_rows + 3
    )
    padded_w = padded_w + marker.astype(jnp.bfloat16)[None]
    high = lax.reduce_precision(local_squares, exponent_bits=8, mantissa_bits=7)
    rest = local_squares - high
    middle = lax.reduce_precision(rest, exponent_bits=8, mantissa_bits=7)
    parts = jnp.zeros((rows_here, 16), jnp.float32).at[:, 0:3].set(
        jnp.stack([high, middle, rest - middle], axis=1)
    )
    widened = jnp.concatenate([hidden, parts.astype(jnp.bfloat16)], axis=1)
    sent = jnp.einsum(
        "gdk,tk->gdt", padded_w, widened, preferred_element_type=jnp.float32
    ).astype(jnp.bfloat16)
    cores = lax.axis_size("core")
    paired = lax.all_to_all(
        sent.reshape(groups // cores, cores, block_rows + 16, rows_here), "core", 1, 1, tiled=False
    )
    paired = jnp.sum(paired.astype(jnp.float32), axis=1)
    pair_squares = jnp.sum(paired[:, block_rows : block_rows + 3], axis=1)
    pair_high = lax.reduce_precision(pair_squares, exponent_bits=8, mantissa_bits=7)
    pair_rest = pair_squares - pair_high
    pair_middle = lax.reduce_precision(pair_rest, exponent_bits=8, mantissa_bits=7)
    paired = paired.at[:, block_rows : block_rows + 3].set(
        jnp.stack([pair_high, pair_middle, pair_rest - pair_middle], axis=1)
    )
    arrived = lax.all_to_all(paired.astype(jnp.bfloat16), "x", 0, 0, tiled=False)
    proj = jnp.sum(arrived[:, :block_rows].astype(jnp.float32), axis=0)
    squares = jnp.sum(arrived[:, block_rows : block_rows + 3].astype(jnp.float32), axis=(0, 1))
    mean_sq = squares / (channels * groups)
    proj = proj * lax.rsqrt(mean_sq + EPS)[None, :]
    block_out = (resid.astype(jnp.float32) + proj).astype(jnp.bfloat16)
    features = resid.shape[0] * groups
    masked_here = masked_pos.shape[0]
    slot_cap = 2 * masked_here // seq_count
    local_pos = masked_pos % rows_here
    owner_hot = (owner[:, None] == jnp.arange(seq_count, dtype=jnp.int32)[None, :]).astype(
        jnp.bfloat16
    )
    strictly = (jnp.arange(masked_here)[:, None] > jnp.arange(masked_here)[None, :]).astype(
        jnp.bfloat16
    )
    earlier = jnp.dot(strictly, owner_hot, preferred_element_type=jnp.float32)
    ranks = jnp.sum(earlier * owner_hot.astype(jnp.float32), axis=-1).astype(jnp.int32)
    placed = owner * slot_cap + ranks
    local_feat = resid.shape[0]
    out_wide = block_out.astype(jnp.float32)
    totals = lax.psum((jnp.sum(out_wide, axis=0), jnp.sum(out_wide * out_wide, axis=0)), ("x", "core"))
    mean_col = totals[0] / features
    variance = totals[1] / features - mean_col * mean_col
    normed = ((out_wide - mean_col[None, :]) * lax.rsqrt(variance + EPS)[None, :]).astype(
        jnp.bfloat16
    )
    pos_hot = (local_pos[:, None] == jnp.arange(rows_here)[None, :]).astype(jnp.bfloat16)
    slot_hot = (placed[:, None] == jnp.arange(seq_count * slot_cap)[None, :]).astype(jnp.bfloat16)
    select = jnp.einsum("jp,js->ps", pos_hot, slot_hot, preferred_element_type=jnp.float32)
    buffer = jnp.dot(
        normed, select.astype(jnp.bfloat16), preferred_element_type=jnp.float32
    ).astype(jnp.bfloat16)
    received = lax.all_to_all(
        buffer.reshape(local_feat, seq_count, slot_cap),
        "seq",
        split_axis=1,
        concat_axis=1,
        tiled=True,
    )
    targets = received.reshape(local_feat, seq_count * slot_cap)
    return (block_out, targets)


def solution(mesh):
    heads = mesh.shape["head"]
    split_mesh = Mesh(
        mesh.devices.reshape(mesh.shape["seq"], heads // 2, 2), ("seq", "x", "core")
    )
    placed = (
        P("seq", ("x", "core")),
        P("seq", ("x", "core")),
        P(("x", "core"), "seq"),
        P(("x", "core"), "seq"),
        P("seq", None),
        P("seq", None),
        P(("x", "core")),
        P(("x", "core")),
        P(("x", "core"), None),
        P(("x", "core"), "seq"),
        P("seq"),
        P("seq"),
    )
    return jax.shard_map(
        body,
        mesh=split_mesh,
        in_specs=placed,
        out_specs=(P(("x", "core"), "seq"), P(("x", "core"), "seq")),
        check_vma=False,
    )
```

```python
import jax
import jax.numpy as jnp
from jax import lax
from jax.sharding import Mesh, PartitionSpec as P

BLOCK = 256


EPS = 1e-05


def from_behind(value, axis, steps):
    count = lax.axis_size(axis)
    leading, last = (max(0, -steps), min(count, count - steps))
    return lax.ppermute(value, axis, [(source, source + steps) for source in range(leading, last)])


def body(
    x_in,
    z_gate,
    step_size,
    log_decay,
    b_proj,
    c_proj,
    d_skip,
    norm_weight,
    w_out,
    resid,
    masked_pos,
    owner,
):
    rows_here = x_in.shape[0]
    heads_here = step_size.shape[0]
    channels = x_in.shape[1]
    head_size = channels // heads_here
    state_size = b_proj.shape[1]
    blocks = rows_here // BLOCK
    x_all = x_in.reshape(blocks, BLOCK, heads_here, head_size)
    b_all = b_proj.reshape(blocks, BLOCK, state_size)
    c_all = c_proj.reshape(blocks, BLOCK, state_size)
    dt_all = step_size.reshape(heads_here, blocks, BLOCK)
    cum_all = jnp.cumsum(log_decay.reshape(heads_here, blocks, BLOCK), axis=-1)
    lower = jnp.arange(BLOCK)[:, None] >= jnp.arange(BLOCK)[None, :]
    gram = jnp.einsum("ctn,csn->cts", c_all, b_all, preferred_element_type=jnp.float32)
    spread = cum_all[:, :, :, None] - cum_all[:, :, None, :]
    decay = jnp.where(lower[None, None], jnp.exp(jnp.where(lower[None, None], spread, 0.0)), 0.0)
    weights = (gram[None] * decay * dt_all[:, :, None, :]).astype(jnp.bfloat16)
    inner = jnp.einsum("hcts,cshp->cthp", weights, x_all, preferred_element_type=jnp.float32)
    end_weight = jnp.exp(cum_all[:, :, -1:] - cum_all) * dt_all
    keyed = (end_weight[..., None] * b_all.astype(jnp.float32)[None]).astype(jnp.bfloat16)
    block_states = jnp.einsum("hcsn,cshp->chpn", keyed, x_all, preferred_element_type=jnp.float32)
    block_decay = jnp.exp(cum_all[:, :, -1])
    running = jnp.zeros((heads_here, head_size, state_size), jnp.float32)
    reach = jnp.ones((heads_here,), jnp.float32)
    starts = []
    reaches = []
    for number in range(blocks):
        starts.append(running)
        reaches.append(reach)
        running = block_decay[:, number][:, None, None] * running + block_states[number]
        reach = reach * block_decay[:, number]
    seq_count = lax.axis_size("seq")
    log_total = jnp.sum(cum_all[:, :, -1], axis=1)
    rows = heads_here * head_size

    def pack(logs, state):
        high = lax.reduce_precision(logs, exponent_bits=8, mantissa_bits=7)
        rest = logs - high
        middle = lax.reduce_precision(rest, exponent_bits=8, mantissa_bits=7)
        spare = jnp.zeros((16, state_size), jnp.float32)
        spare = spare.at[0:3, 0:heads_here].set(jnp.stack([high, middle, rest - middle]))
        return jnp.concatenate([state.reshape(rows, state_size), spare], axis=0).astype(
            jnp.bfloat16
        )

    def unpack(slab):
        wide = slab.astype(jnp.float32)
        logs = jnp.sum(wide[rows : rows + 3, :heads_here], axis=0)
        return logs, wide[:rows].reshape(heads_here, head_size, state_size)

    logs = jnp.zeros_like(log_total)
    state = jnp.zeros_like(running)
    window_logs, window_state = log_total, running
    distance = 1
    while distance < seq_count:
        earlier_logs, earlier_state = unpack(
            from_behind(pack(window_logs, window_state), "seq", distance)
        )
        state = jnp.exp(logs)[:, None, None] * earlier_state + state
        logs = logs + earlier_logs
        distance *= 2
        if distance < seq_count:
            window_state = jnp.exp(log_total)[:, None, None] * state + running
            window_logs = logs + log_total
    incoming = state
    start_states = jnp.stack(starts) + jnp.stack(reaches)[:, :, None, None] * incoming[None]
    carried = jnp.einsum(
        "ctn,chpn->cthp",
        c_all.astype(jnp.float32),
        start_states,
        precision=lax.Precision.HIGHEST,
        preferred_element_type=jnp.float32,
    )
    carried = carried * jnp.transpose(jnp.exp(cum_all), (1, 2, 0))[:, :, :, None]
    mixed = inner + carried + d_skip[None, None, :, None] * x_all.astype(jnp.float32)
    mixed = mixed.reshape(rows_here, channels)
    gated = mixed * jax.nn.silu(z_gate.astype(jnp.float32))
    local_squares = jnp.sum(gated * gated, axis=-1)
    hidden = (gated * norm_weight[None, :]).astype(jnp.bfloat16)
    groups = lax.axis_size("x") * lax.axis_size("core")
    block_rows = w_out.shape[1] // groups
    padded_w = jnp.pad(
        jnp.transpose(w_out.reshape(w_out.shape[0], groups, block_rows), (1, 2, 0)),
        ((0, 0), (0, 16), (0, 16)),
    )
    out_row = jnp.arange(block_rows + 16)[:, None]
    in_col = jnp.arange(channels + 16)[None, :]
    marker = (out_row - block_rows == in_col - channels) & (out_row >= block_rows) & (
        out_row < block_rows + 3
    )
    padded_w = padded_w + marker.astype(jnp.bfloat16)[None]
    high = lax.reduce_precision(local_squares, exponent_bits=8, mantissa_bits=7)
    rest = local_squares - high
    middle = lax.reduce_precision(rest, exponent_bits=8, mantissa_bits=7)
    parts = jnp.zeros((rows_here, 16), jnp.float32).at[:, 0:3].set(
        jnp.stack([high, middle, rest - middle], axis=1)
    )
    widened = jnp.concatenate([hidden, parts.astype(jnp.bfloat16)], axis=1)
    sent = jnp.einsum(
        "gdk,tk->gdt", padded_w, widened, preferred_element_type=jnp.float32
    ).astype(jnp.bfloat16)
    cores = lax.axis_size("core")
    paired = lax.all_to_all(
        sent.reshape(groups // cores, cores, block_rows + 16, rows_here), "core", 1, 1, tiled=False
    )
    paired = jnp.sum(paired.astype(jnp.float32), axis=1)
    pair_squares = jnp.sum(paired[:, block_rows : block_rows + 3], axis=1)
    pair_high = lax.reduce_precision(pair_squares, exponent_bits=8, mantissa_bits=7)
    pair_rest = pair_squares - pair_high
    pair_middle = lax.reduce_precision(pair_rest, exponent_bits=8, mantissa_bits=7)
    paired = paired.at[:, block_rows : block_rows + 3].set(
        jnp.stack([pair_high, pair_middle, pair_rest - pair_middle], axis=1)
    )
    arrived = lax.all_to_all(paired.astype(jnp.bfloat16), "x", 0, 0, tiled=False)
    proj = jnp.sum(arrived[:, :block_rows].astype(jnp.float32), axis=0)
    squares = jnp.sum(arrived[:, block_rows : block_rows + 3].astype(jnp.float32), axis=(0, 1))
    mean_sq = squares / (channels * groups)
    proj = proj * lax.rsqrt(mean_sq + EPS)[None, :]
    block_out = (resid.astype(jnp.float32) + proj).astype(jnp.bfloat16)
    features = resid.shape[0] * groups
    masked_here = masked_pos.shape[0]
    slot_cap = 2 * masked_here // seq_count
    local_pos = masked_pos % rows_here
    owner_hot = (owner[:, None] == jnp.arange(seq_count, dtype=jnp.int32)[None, :]).astype(
        jnp.bfloat16
    )
    strictly = (jnp.arange(masked_here)[:, None] > jnp.arange(masked_here)[None, :]).astype(
        jnp.bfloat16
    )
    earlier = jnp.dot(strictly, owner_hot, preferred_element_type=jnp.float32)
    ranks = jnp.sum(earlier * owner_hot.astype(jnp.float32), axis=-1).astype(jnp.int32)
    placed = owner * slot_cap + ranks
    local_feat = resid.shape[0]
    out_wide = block_out.astype(jnp.float32)
    totals = lax.psum(
        lax.psum((jnp.sum(out_wide, axis=0), jnp.sum(out_wide * out_wide, axis=0)), "core"), "x"
    )
    mean_col = totals[0] / features
    variance = totals[1] / features - mean_col * mean_col
    normed = ((out_wide - mean_col[None, :]) * lax.rsqrt(variance + EPS)[None, :]).astype(
        jnp.bfloat16
    )
    pos_hot = (local_pos[:, None] == jnp.arange(rows_here)[None, :]).astype(jnp.bfloat16)
    slot_hot = (placed[:, None] == jnp.arange(seq_count * slot_cap)[None, :]).astype(jnp.bfloat16)
    select = jnp.einsum("jp,js->ps", pos_hot, slot_hot, preferred_element_type=jnp.float32)
    buffer = jnp.dot(
        normed, select.astype(jnp.bfloat16), preferred_element_type=jnp.float32
    ).astype(jnp.bfloat16)
    received = lax.all_to_all(
        buffer.reshape(local_feat, seq_count, slot_cap),
        "seq",
        split_axis=1,
        concat_axis=1,
        tiled=True,
    )
    targets = received.reshape(local_feat, seq_count * slot_cap)
    return (block_out, targets)


def solution(mesh):
    heads = mesh.shape["head"]
    split_mesh = Mesh(
        mesh.devices.reshape(mesh.shape["seq"], heads // 2, 2), ("seq", "x", "core")
    )
    placed = (
        P("seq", ("x", "core")),
        P("seq", ("x", "core")),
        P(("x", "core"), "seq"),
        P(("x", "core"), "seq"),
        P("seq", None),
        P("seq", None),
        P(("x", "core")),
        P(("x", "core")),
        P(("x", "core"), None),
        P(("x", "core"), "seq"),
        P("seq"),
        P("seq"),
    )
    return jax.shard_map(
        body,
        mesh=split_mesh,
        in_specs=placed,
        out_specs=(P(("x", "core"), "seq"), P(("x", "core"), "seq")),
        check_vma=False,
    )
```

```python
import jax
import jax.numpy as jnp
from jax import lax
from jax.sharding import Mesh, PartitionSpec as P

BLOCK = 256


EPS = 1e-05


def from_behind(value, axis, steps):
    count = lax.axis_size(axis)
    leading, last = (max(0, -steps), min(count, count - steps))
    return lax.ppermute(value, axis, [(source, source + steps) for source in range(leading, last)])


def body(
    x_in,
    z_gate,
    step_size,
    log_decay,
    b_proj,
    c_proj,
    d_skip,
    norm_weight,
    w_out,
    resid,
    masked_pos,
    owner,
):
    rows_here = x_in.shape[0]
    heads_here = step_size.shape[0]
    channels = x_in.shape[1]
    head_size = channels // heads_here
    state_size = b_proj.shape[1]
    blocks = rows_here // BLOCK
    x_all = x_in.reshape(blocks, BLOCK, heads_here, head_size)
    b_all = b_proj.reshape(blocks, BLOCK, state_size)
    c_all = c_proj.reshape(blocks, BLOCK, state_size)
    dt_all = step_size.reshape(heads_here, blocks, BLOCK)
    cum_all = jnp.cumsum(log_decay.reshape(heads_here, blocks, BLOCK), axis=-1)
    lower = jnp.arange(BLOCK)[:, None] >= jnp.arange(BLOCK)[None, :]
    gram = jnp.einsum("ctn,csn->cts", c_all, b_all, preferred_element_type=jnp.float32)
    spread = cum_all[:, :, :, None] - cum_all[:, :, None, :]
    decay = jnp.where(lower[None, None], jnp.exp(jnp.where(lower[None, None], spread, 0.0)), 0.0)
    weights = (gram[None] * decay * dt_all[:, :, None, :]).astype(jnp.bfloat16)
    inner = jnp.einsum("hcts,cshp->cthp", weights, x_all, preferred_element_type=jnp.float32)
    end_weight = jnp.exp(cum_all[:, :, -1:] - cum_all) * dt_all
    keyed = (end_weight[..., None] * b_all.astype(jnp.float32)[None]).astype(jnp.bfloat16)
    block_states = jnp.einsum("hcsn,cshp->chpn", keyed, x_all, preferred_element_type=jnp.float32)
    block_decay = jnp.exp(cum_all[:, :, -1])
    running = jnp.zeros((heads_here, head_size, state_size), jnp.float32)
    reach = jnp.ones((heads_here,), jnp.float32)
    starts = []
    reaches = []
    for number in range(blocks):
        starts.append(running)
        reaches.append(reach)
        running = block_decay[:, number][:, None, None] * running + block_states[number]
        reach = reach * block_decay[:, number]
    seq_count = lax.axis_size("seq")
    log_total = jnp.sum(cum_all[:, :, -1], axis=1)
    rows = heads_here * head_size

    def pack(logs, state):
        high = lax.reduce_precision(logs, exponent_bits=8, mantissa_bits=7)
        rest = logs - high
        middle = lax.reduce_precision(rest, exponent_bits=8, mantissa_bits=7)
        spare = jnp.zeros((16, state_size), jnp.float32)
        spare = spare.at[0:3, 0:heads_here].set(jnp.stack([high, middle, rest - middle]))
        return jnp.concatenate([state.reshape(rows, state_size), spare], axis=0).astype(
            jnp.bfloat16
        )

    def unpack(slab):
        wide = slab.astype(jnp.float32)
        logs = jnp.sum(wide[rows : rows + 3, :heads_here], axis=0)
        return logs, wide[:rows].reshape(heads_here, head_size, state_size)

    logs = jnp.zeros_like(log_total)
    state = jnp.zeros_like(running)
    window_logs, window_state = log_total, running
    distance = 1
    while distance < seq_count:
        earlier_logs, earlier_state = unpack(
            from_behind(pack(window_logs, window_state), "seq", distance)
        )
        state = jnp.exp(logs)[:, None, None] * earlier_state + state
        logs = logs + earlier_logs
        distance *= 2
        if distance < seq_count:
            window_state = jnp.exp(log_total)[:, None, None] * state + running
            window_logs = logs + log_total
    incoming = state
    start_states = jnp.stack(starts) + jnp.stack(reaches)[:, :, None, None] * incoming[None]
    carried = jnp.einsum(
        "ctn,chpn->cthp",
        c_all.astype(jnp.float32),
        start_states,
        precision=lax.Precision.HIGHEST,
        preferred_element_type=jnp.float32,
    )
    carried = carried * jnp.transpose(jnp.exp(cum_all), (1, 2, 0))[:, :, :, None]
    mixed = inner + carried + d_skip[None, None, :, None] * x_all.astype(jnp.float32)
    mixed = mixed.reshape(rows_here, channels)
    gated = mixed * jax.nn.silu(z_gate.astype(jnp.float32))
    local_squares = jnp.sum(gated * gated, axis=-1)
    hidden = (gated * norm_weight[None, :]).astype(jnp.bfloat16)
    groups = lax.axis_size("x") * lax.axis_size("core")
    block_rows = w_out.shape[1] // groups
    padded_w = jnp.pad(
        jnp.transpose(w_out.reshape(w_out.shape[0], groups, block_rows), (1, 2, 0)),
        ((0, 0), (0, 16), (0, 16)),
    )
    out_row = jnp.arange(block_rows + 16)[:, None]
    in_col = jnp.arange(channels + 16)[None, :]
    marker = (out_row - block_rows == in_col - channels) & (out_row >= block_rows) & (
        out_row < block_rows + 3
    )
    padded_w = padded_w + marker.astype(jnp.bfloat16)[None]
    high = lax.reduce_precision(local_squares, exponent_bits=8, mantissa_bits=7)
    rest = local_squares - high
    middle = lax.reduce_precision(rest, exponent_bits=8, mantissa_bits=7)
    parts = jnp.zeros((rows_here, 16), jnp.float32).at[:, 0:3].set(
        jnp.stack([high, middle, rest - middle], axis=1)
    )
    widened = jnp.concatenate([hidden, parts.astype(jnp.bfloat16)], axis=1)
    cores = lax.axis_size("core")
    core = lax.axis_index("core")
    by_core = padded_w.reshape(groups // cores, cores, block_rows + 16, channels + 16)
    other_w = lax.dynamic_index_in_dim(by_core, cores - 1 - core, axis=1, keepdims=False)
    own_w = lax.dynamic_index_in_dim(by_core, core, axis=1, keepdims=False)
    to_partner = jnp.einsum(
        "gdk,tk->gdt", other_w, widened, preferred_element_type=jnp.float32
    ).astype(jnp.bfloat16)
    from_partner = lax.ppermute(to_partner, "core", [(0, 1), (1, 0)])
    own_part = jnp.einsum(
        "gdk,tk->gdt", own_w, widened, preferred_element_type=jnp.float32
    ).astype(jnp.bfloat16)
    paired = own_part.astype(jnp.float32) + from_partner.astype(jnp.float32)
    pair_squares = jnp.sum(paired[:, block_rows : block_rows + 3], axis=1)
    pair_high = lax.reduce_precision(pair_squares, exponent_bits=8, mantissa_bits=7)
    pair_rest = pair_squares - pair_high
    pair_middle = lax.reduce_precision(pair_rest, exponent_bits=8, mantissa_bits=7)
    paired = paired.at[:, block_rows : block_rows + 3].set(
        jnp.stack([pair_high, pair_middle, pair_rest - pair_middle], axis=1)
    )
    arrived = lax.all_to_all(paired.astype(jnp.bfloat16), "x", 0, 0, tiled=False)
    proj = jnp.sum(arrived[:, :block_rows].astype(jnp.float32), axis=0)
    squares = jnp.sum(arrived[:, block_rows : block_rows + 3].astype(jnp.float32), axis=(0, 1))
    mean_sq = squares / (channels * groups)
    proj = proj * lax.rsqrt(mean_sq + EPS)[None, :]
    block_out = (resid.astype(jnp.float32) + proj).astype(jnp.bfloat16)
    features = resid.shape[0] * groups
    masked_here = masked_pos.shape[0]
    slot_cap = 2 * masked_here // seq_count
    local_pos = masked_pos % rows_here
    owner_hot = (owner[:, None] == jnp.arange(seq_count, dtype=jnp.int32)[None, :]).astype(
        jnp.bfloat16
    )
    strictly = (jnp.arange(masked_here)[:, None] > jnp.arange(masked_here)[None, :]).astype(
        jnp.bfloat16
    )
    earlier = jnp.dot(strictly, owner_hot, preferred_element_type=jnp.float32)
    ranks = jnp.sum(earlier * owner_hot.astype(jnp.float32), axis=-1).astype(jnp.int32)
    placed = owner * slot_cap + ranks
    local_feat = resid.shape[0]
    out_wide = block_out.astype(jnp.float32)
    totals = lax.psum(
        lax.psum((jnp.sum(out_wide, axis=0), jnp.sum(out_wide * out_wide, axis=0)), "core"), "x"
    )
    mean_col = totals[0] / features
    variance = totals[1] / features - mean_col * mean_col
    normed = ((out_wide - mean_col[None, :]) * lax.rsqrt(variance + EPS)[None, :]).astype(
        jnp.bfloat16
    )
    pos_hot = (local_pos[:, None] == jnp.arange(rows_here)[None, :]).astype(jnp.bfloat16)
    slot_hot = (placed[:, None] == jnp.arange(seq_count * slot_cap)[None, :]).astype(jnp.bfloat16)
    select = jnp.einsum("jp,js->ps", pos_hot, slot_hot, preferred_element_type=jnp.float32)
    buffer = jnp.dot(
        normed, select.astype(jnp.bfloat16), preferred_element_type=jnp.float32
    ).astype(jnp.bfloat16)
    received = lax.all_to_all(
        buffer.reshape(local_feat, seq_count, slot_cap),
        "seq",
        split_axis=1,
        concat_axis=1,
        tiled=True,
    )
    targets = received.reshape(local_feat, seq_count * slot_cap)
    return (block_out, targets)


def solution(mesh):
    heads = mesh.shape["head"]
    split_mesh = Mesh(
        mesh.devices.reshape(mesh.shape["seq"], heads // 2, 2), ("seq", "x", "core")
    )
    placed = (
        P("seq", ("x", "core")),
        P("seq", ("x", "core")),
        P(("x", "core"), "seq"),
        P(("x", "core"), "seq"),
        P("seq", None),
        P("seq", None),
        P(("x", "core")),
        P(("x", "core")),
        P(("x", "core"), None),
        P(("x", "core"), "seq"),
        P("seq"),
        P("seq"),
    )
    return jax.shard_map(
        body,
        mesh=split_mesh,
        in_specs=placed,
        out_specs=(P(("x", "core"), "seq"), P(("x", "core"), "seq")),
        check_vma=False,
    )
```
